512 devices in a mesh: rep: 8 (over y, core), expert: 64 (over x, z).
Axes of the slice: x: 4, y: 4, z: 16, core: 2. Of those that a mesh axis runs over, the one named last changes fastest.
Arguments:
- tokens: bfloat16 [8192, 4096], P('expert', 'rep')
- norm_gain: float32 [4096], P('rep'), may hold values from 0.25 to 1.75
- gate_weights: float32 [8192, 8], P('expert'), may hold values from 0.1 to 0.6
- exit_flags: int32 [8192], P('expert'), may hold values from 0 to 1, as said below
- routes: int32 [8192, 8], P('expert'), may hold values from 0 to 127, as said below
- next_device: int32 [8192], P('expert'), may hold values from 0 to 63, as said below
- up_weight: bfloat16 [128, 4096, 1024], P('expert', 'rep'), may hold values from -0.09375 to 0.09375
- down_weight: bfloat16 [128, 1024, 4096], P('expert', None, 'rep'), may hold values from -0.1875 to 0.1875
Outputs:
- handed: float32 [4096, 4096], P('expert', 'rep')
The draws below stay inside these ranges and needn't reach their ends.
Inputs may be any that keep to these rules, and one draw needn't show every extreme that they name: `exit_flags`: one block of 128 rows holds at most 64 live rows; some block holds exactly 64. `routes`: each row names 8 different experts. Among the live rows of one block, every expert is named the same number of times up to one, so at most 4 times; a block with 64 live rows names every expert exactly 4 times. `next_device`: among the live rows of one block, every value is named the same number of times up to one, so at most 1 times.
All inputs are finite; a program needn't handle non-finite values.
Results may differ from the reference program's by a relative error of at most 0.0017.
Values may be sent and summed in bfloat16 or wider, within the bound.
No kernel may reach another device: no remote copies, remote signals or barrier semaphores. Data moves between devices by JAX's collectives and lax.ppermute only.
A program may use at most 64 MiB of HBM per device.

```python
import jax
import jax.numpy as jnp
from jax import lax

D = 4096
HID = 1024
TOP = 8
ROW_DEV = 128
EXPERTS = 128
ROWS = 8192
MAX_SURVIVE_ROWS = 64
CAP = 4
HCAP = 1
HANDED = 4096
N_EXPERT = 64


def plan_rows(key):
    block_list = ROWS // ROW_DEV
    keys = jax.random.split(jax.random.fold_in(key, 71), 5)
    depth_level = jax.random.randint(keys[0], (block_list,), 0, 4)
    surviving_rows = MAX_SURVIVE_ROWS // 8 * jnp.left_shift(1, depth_level)
    forced_exit = jax.random.randint(keys[1], (), 0, block_list)
    surviving_rows = jnp.where(jnp.arange(block_list) == forced_exit, MAX_SURVIVE_ROWS, surviving_rows)
    sorted_order = jax.vmap(lambda single: jax.random.permutation(single, ROW_DEV))(jax.random.split(keys[2], block_list))
    alive_mask = (sorted_order < surviving_rows[:, None]).astype(jnp.int32)
    live_rank = jnp.cumsum(alive_mask, axis=1) - alive_mask
    dead_rank = jnp.cumsum(1 - alive_mask, axis=1) - (1 - alive_mask)
    return (alive_mask, live_rank, dead_rank, keys[3], keys[4])


def draw_exit_flags(key, part):
    alive_mask, live_rank, dead_rank, key_route, key_dest = plan_rows(key)
    return (1 - alive_mask).reshape(ROWS).astype(jnp.int32)


def draw_routes(key, part):
    alive_mask, live_rank, dead_rank, key_route, key_dest = plan_rows(key)
    block_list = ROWS // ROW_DEV
    perms = jax.vmap(lambda single: jax.random.permutation(single, EXPERTS))(jax.random.split(key_route, block_list * CAP))
    perms = perms.reshape(block_list, CAP, EXPERTS)
    slot_k = jnp.arange(TOP)[None, None, :]
    live_pair = live_rank[:, :, None] * TOP + slot_k
    dead_pair = dead_rank[:, :, None] * TOP + slot_k
    alive_b = alive_mask[:, :, None] > 0
    round_idx = jnp.where(alive_b, live_pair // EXPERTS, 0)
    column = jnp.where(alive_b, live_pair % EXPERTS, dead_pair % EXPERTS)
    block_idx = jnp.broadcast_to(jnp.arange(block_list)[:, None, None], column.shape)
    chosen = perms[block_idx, round_idx, column]
    return chosen.reshape(ROWS, TOP).astype(jnp.int32)


def draw_next_device(key, part):
    alive_mask, live_rank, dead_rank, key_route, key_dest = plan_rows(key)
    block_list = ROWS // ROW_DEV
    perms = jax.vmap(lambda single: jax.random.permutation(single, N_EXPERT))(jax.random.split(key_dest, block_list))
    index = jnp.where(alive_mask > 0, live_rank, dead_rank) % N_EXPERT
    block_idx = jnp.broadcast_to(jnp.arange(block_list)[:, None], index.shape)
    return perms[block_idx, index].reshape(ROWS).astype(jnp.int32)


def draw_tokens(key, part):
    keys = jax.random.split(jax.random.fold_in(key, 5), 4)
    column_pos = jnp.arange(D, dtype=jnp.float32) / D
    column_scale = 10.0 ** (jax.random.uniform(keys[0], (D,)) - 0.5) * 3.0 ** (0.6 * column_pos - 0.3)
    row_scale = 10.0 ** (jax.random.uniform(keys[1], (ROWS,)) - 0.5)
    base = jnp.clip(jax.random.normal(keys[3], (ROWS, D)), -4.0, 4.0)
    values = row_scale[:, None] * column_scale[None, :] * base
    return values.astype(jnp.float32).astype(jnp.bfloat16)


def shard_levels(stream_key, dims, shards, smallest, top_value):
    def one(dim, parts):
        heights = jax.random.uniform(jax.random.fold_in(jax.random.fold_in(stream_key, 6), dim), (parts,), jnp.float32, smallest / len(shards), top_value / len(shards))
        return jnp.repeat(jnp.exp(heights), dims[dim] // parts).reshape((-1,) + (1,) * (len(dims) - dim - 1))

    level = one(*shards[0])
    for cut in shards[1:]:
        level = level * one(*cut)
    return level


def noise(rng, shape, scale, reach, cuts=(), kind=jnp.bfloat16):
    array = scale * jax.random.normal(rng, shape, jnp.float32)
    if cuts:
        array = array * shard_levels(rng, shape, cuts, -0.22, 0.18)
    return jnp.clip(array, -reach, reach).astype(kind)


def setup_inputs(seed: int = 0) -> dict:
    splits = jax.random.split(jax.random.key(seed), 9)
    return {
        "tokens": draw_tokens(jax.random.fold_in(splits[8], 71), 0),
        "norm_gain": jnp.clip(1.0 + 0.15 * jax.random.normal(splits[1], (D,), jnp.float32), 0.25, 1.75),
        "gate_weights": jnp.clip(0.1 + 0.5 * jax.random.uniform(splits[2], (ROWS, TOP), jnp.float32) ** shard_levels(splits[2], (ROWS, TOP), ((0, 64),), -0.2, 0.2), 0.1, 0.6),
        "exit_flags": draw_exit_flags(jax.random.fold_in(splits[8], 71), 0),
        "routes": draw_routes(jax.random.fold_in(splits[8], 71), 0),
        "next_device": draw_next_device(jax.random.fold_in(splits[8], 71), 0),
        "up_weight": noise(splits[6], (EXPERTS, D, HID), D ** -0.5, 0.09375, ((0, 64), (1, 8))),
        "down_weight": noise(splits[7], (EXPERTS, HID, D), HID ** -0.5, 0.1875, ((0, 64), (2, 8))),
    }


def reference(tokens, norm_gain, gate_weights, exit_flags, routes, next_device, up_weight, down_weight):
    widened = tokens.astype(jnp.float32)
    rinv_rows = lax.rsqrt(lax.optimization_barrier(jnp.sum(widened * widened, axis=1)) / D + 1e-06)
    normed = (widened * rinv_rows[:, None] * norm_gain[None, :]).astype(jnp.bfloat16)
    survive = (1 - exit_flags).astype(jnp.int32)
    pair_live = jnp.repeat(survive, TOP)
    route_flat = routes.reshape(-1).astype(jnp.int32)
    one_hot = (route_flat[:, None] == jnp.arange(EXPERTS, dtype=jnp.int32)[None, :]).astype(jnp.int32) * pair_live[:, None]
    blocked = one_hot.reshape(N_EXPERT, ROW_DEV * TOP, EXPERTS)
    earlier = (jnp.cumsum(blocked, axis=1) - blocked).reshape(ROWS * TOP, EXPERTS)
    position = lax.optimization_barrier(jnp.sum(earlier * one_hot, axis=1)).astype(jnp.int32)
    source_dev = jnp.arange(ROWS * TOP, dtype=jnp.int32) // (ROW_DEV * TOP)
    slot_index = jnp.where(pair_live > 0, source_dev * CAP + position, N_EXPERT * CAP).astype(jnp.int32)
    row_plus = (jnp.arange(ROWS * TOP, dtype=jnp.int32) // TOP + 1).astype(jnp.int32)
    table = jnp.zeros((EXPERTS, N_EXPERT * CAP), jnp.int32).at[route_flat, slot_index].set(row_plus, mode='drop')
    padded = jnp.concatenate([jnp.zeros((1, D), jnp.bfloat16), normed], axis=0)

    def per_expert(items):
        w_up, w_down, row_ids = items
        gathered = padded[row_ids]
        hidden = jnp.dot(gathered, w_up, preferred_element_type=jnp.float32)
        activated = jax.nn.silu(hidden).astype(jnp.bfloat16)
        return jnp.dot(activated, w_down, preferred_element_type=jnp.float32).astype(jnp.bfloat16)
    expert_out = lax.map(per_expert, (up_weight, down_weight, table)).reshape(EXPERTS * N_EXPERT * CAP, D)
    chosen = (route_flat * (N_EXPERT * CAP) + jnp.minimum(slot_index, N_EXPERT * CAP - 1)).reshape(ROWS, TOP)
    mixture = jnp.zeros((ROWS, D), jnp.float32)
    for slot_k in range(TOP):
        mixture = mixture + gate_weights[:, slot_k:slot_k + 1] * expert_out[chosen[:, slot_k]].astype(jnp.float32)
    updated = widened + mixture
    dest_hot = (next_device[:, None] == jnp.arange(N_EXPERT, dtype=jnp.int32)[None, :]).astype(jnp.int32) * survive[:, None]
    dest_block = dest_hot.reshape(N_EXPERT, ROW_DEV, N_EXPERT)
    dest_before = (jnp.cumsum(dest_block, axis=1) - dest_block).reshape(ROWS, N_EXPERT)
    handoff_pos = lax.optimization_barrier(jnp.sum(dest_before * dest_hot, axis=1)).astype(jnp.int32)
    source_row_dev = jnp.arange(ROWS, dtype=jnp.int32) // ROW_DEV
    target = next_device * (N_EXPERT * HCAP) + source_row_dev * HCAP + handoff_pos
    target = jnp.where(survive > 0, target, HANDED).astype(jnp.int32)
    return jnp.zeros((HANDED, D), jnp.float32).at[target].set(updated, mode='drop')
```

```python
import jax
import jax.numpy as jnp
from jax import lax
from jax.sharding import PartitionSpec as P


def per_device(
    tokens, norm_gain, gate_weights, exit_flags, routes, next_device, up_weight, down_weight
):
    row_count, feat_width = tokens.shape
    owner_count = lax.axis_size("expert")
    rep_count = lax.axis_size("rep")
    local_experts = up_weight.shape[0]
    hid = up_weight.shape[2]
    route_count = routes.shape[1]
    experts_all = local_experts * owner_count
    most_live = row_count // 2
    capacity = route_count * most_live // experts_all
    hand_cap = (most_live + owner_count - 1) // owner_count
    slot_total = local_experts * owner_count * capacity
    hid_part = hid // rep_count
    widened = tokens.astype(jnp.float32)
    survive = 1 - exit_flags
    pair_live = jnp.repeat(survive, route_count)
    route_flat = routes.reshape(-1)
    one_hot = (route_flat[:, None] == jnp.arange(experts_all, dtype=jnp.int32)[None, :]).astype(
        jnp.int32
    ) * pair_live[:, None]
    earlier = jnp.cumsum(one_hot, axis=0) - one_hot
    position = jnp.sum(earlier * one_hot, axis=1)
    owner_id = route_flat // local_experts
    local_id = route_flat % local_experts
    slot_index = (local_id * owner_count + owner_id) * capacity + position
    slot_index = jnp.where(pair_live > 0, slot_index, slot_total)
    pair_row = jnp.arange(row_count * route_count, dtype=jnp.int32) // route_count
    source_row = jnp.zeros((slot_total,), jnp.int32).at[slot_index].set(pair_row + 1, mode="drop")
    padded = jnp.concatenate([jnp.zeros((1, feat_width), jnp.bfloat16), tokens], axis=0)
    outbound = padded[source_row].reshape(local_experts, owner_count, capacity, feat_width)
    received = lax.all_to_all(outbound, "expert", split_axis=1, concat_axis=1, tiled=True)
    item_count = received.shape[2]
    rows_here = owner_count * item_count
    flattened = received.reshape(local_experts, rows_here, feat_width).astype(jnp.float32)
    scaled = flattened * norm_gain[None, None, :]
    high = scaled.astype(jnp.bfloat16)
    low = (scaled - high.astype(jnp.float32)).astype(jnp.bfloat16)
    partial_value = jnp.einsum(
        "erd,edh->erh", high, up_weight, preferred_element_type=jnp.float32
    ) + jnp.einsum("erd,edh->erh", low, up_weight, preferred_element_type=jnp.float32)
    squares = jnp.sum(flattened * flattened, axis=2)
    pieces = partial_value.reshape(local_experts * rows_here, rep_count, hid_part)
    pieces = jnp.transpose(pieces, (1, 0, 2))
    sq_rows = squares.reshape(-1, hid_part)
    sq_tile = jnp.broadcast_to(sq_rows[None], (rep_count,) + sq_rows.shape)
    packed = jnp.concatenate([pieces, sq_tile], axis=1)
    got = lax.all_to_all(packed, "rep", split_axis=0, concat_axis=0, tiled=True)
    total = jnp.sum(got, axis=0)
    hidden_part = total[: local_experts * rows_here].reshape(local_experts, rows_here, hid_part)
    sq_total = total[local_experts * rows_here :].reshape(local_experts, rows_here)
    rinv = lax.rsqrt(sq_total / (feat_width * rep_count) + 1e-06)
    hidden_part = hidden_part * rinv[:, :, None]
    act_part = jax.nn.silu(hidden_part).astype(jnp.bfloat16)
    act_tile = jnp.broadcast_to(act_part[None], (rep_count,) + act_part.shape)
    act_all = lax.all_to_all(act_tile, "rep", split_axis=0, concat_axis=0, tiled=True)
    activated = jnp.transpose(act_all, (1, 2, 0, 3)).reshape(local_experts, rows_here, hid)
    expert_out = jnp.einsum(
        "erh,ehd->erd", activated, down_weight, preferred_element_type=jnp.float32
    )
    expert_out = expert_out.astype(jnp.bfloat16).reshape(
        local_experts, owner_count, item_count, feat_width
    )
    returned = lax.all_to_all(expert_out, "expert", split_axis=1, concat_axis=1, tiled=True)
    flat_back = returned.reshape(slot_total, feat_width)
    picked = flat_back[jnp.minimum(slot_index, slot_total - 1)].reshape(
        row_count, route_count, feat_width
    )
    mixture = jnp.einsum("rk,rkd->rd", gate_weights, picked, preferred_element_type=jnp.float32)
    updated = widened + mixture
    dest_hot = (next_device[:, None] == jnp.arange(owner_count, dtype=jnp.int32)[None, :]).astype(
        jnp.int32
    ) * survive[:, None]
    dest_before = jnp.cumsum(dest_hot, axis=0) - dest_hot
    handoff_pos = jnp.sum(dest_before * dest_hot, axis=1)
    hand_slot = jnp.where(survive > 0, next_device * hand_cap + handoff_pos, owner_count * hand_cap)
    row_plus = jnp.arange(row_count, dtype=jnp.int32) + 1
    target = (
        jnp.zeros((owner_count * hand_cap,), jnp.int32).at[hand_slot].set(row_plus, mode="drop")
    )
    stacked = jnp.concatenate([jnp.zeros((1, feat_width), jnp.float32), updated], axis=0)
    leaving = stacked[target].reshape(owner_count, hand_cap, feat_width)
    arrived = lax.all_to_all(leaving, "expert", split_axis=0, concat_axis=0, tiled=True)
    return arrived.reshape(owner_count * hand_cap, feat_width)


def solution(mesh):
    in_specs = (
        P("expert", "rep"),
        P("rep"),
        P("expert", None),
        P("expert"),
        P("expert", None),
        P("expert"),
        P("expert", "rep", None),
        P("expert", None, "rep"),
    )
    out_specs = P("expert", "rep")
    return jax.shard_map(
        per_device, mesh=mesh, in_specs=in_specs, out_specs=out_specs, check_vma=False
    )
```

```python
import jax
import jax.numpy as jnp
from jax import lax
from jax.sharding import PartitionSpec as P


def per_device(
    tokens, norm_gain, gate_weights, exit_flags, routes, next_device, up_weight, down_weight
):
    row_count, feat_width = tokens.shape
    owner_count = lax.axis_size("expert")
    rep_count = lax.axis_size("rep")
    local_experts = up_weight.shape[0]
    hid = up_weight.shape[2]
    route_count = routes.shape[1]
    experts_all = local_experts * owner_count
    most_live = row_count // 2
    capacity = route_count * most_live // experts_all
    hand_cap = (most_live + owner_count - 1) // owner_count
    slot_total = local_experts * owner_count * capacity
    hid_part = hid // rep_count
    widened = tokens.astype(jnp.float32)
    survive = 1 - exit_flags
    pair_live = jnp.repeat(survive, route_count)
    route_flat = routes.reshape(-1)
    one_hot = (route_flat[:, None] == jnp.arange(experts_all, dtype=jnp.int32)[None, :]).astype(
        jnp.int32
    ) * pair_live[:, None]
    earlier = jnp.cumsum(one_hot, axis=0) - one_hot
    position = jnp.sum(earlier * one_hot, axis=1)
    owner_id = route_flat // local_experts
    local_id = route_flat % local_experts
    slot_index = (local_id * owner_count + owner_id) * capacity + position
    slot_index = jnp.where(pair_live > 0, slot_index, slot_total)
    pair_row = jnp.arange(row_count * route_count, dtype=jnp.int32) // route_count
    source_row = jnp.zeros((slot_total,), jnp.int32).at[slot_index].set(pair_row + 1, mode="drop")
    squares = lax.psum(jnp.sum(widened * widened, axis=1), "rep")
    rinv_rows = lax.rsqrt(squares / (feat_width * rep_count) + 1e-06)
    normed = (widened * rinv_rows[:, None] * norm_gain[None, :]).astype(jnp.bfloat16)
    padded = jnp.concatenate([jnp.zeros((1, feat_width), jnp.bfloat16), normed], axis=0)
    outbound = padded[source_row].reshape(local_experts, owner_count, capacity, feat_width)
    received = lax.all_to_all(outbound, "expert", split_axis=1, concat_axis=1, tiled=True)
    item_count = received.shape[2]
    rows_here = owner_count * item_count
    flattened = received.reshape(local_experts, rows_here, feat_width)
    partial_value = jnp.einsum(
        "erd,edh->erh", flattened, up_weight, preferred_element_type=jnp.float32
    )
    pieces = partial_value.reshape(local_experts * rows_here, rep_count, hid_part)
    pieces = jnp.transpose(pieces, (1, 0, 2))
    got = lax.all_to_all(pieces, "rep", split_axis=0, concat_axis=0, tiled=True)
    hidden_part = jnp.sum(got, axis=0).reshape(local_experts, rows_here, hid_part)
    act_part = jax.nn.silu(hidden_part).astype(jnp.bfloat16)
    act_tile = jnp.broadcast_to(act_part[None], (rep_count,) + act_part.shape)
    act_all = lax.all_to_all(act_tile, "rep", split_axis=0, concat_axis=0, tiled=True)
    activated = jnp.transpose(act_all, (1, 2, 0, 3)).reshape(local_experts, rows_here, hid)
    expert_out = jnp.einsum(
        "erh,ehd->erd", activated, down_weight, preferred_element_type=jnp.float32
    )
    expert_out = expert_out.astype(jnp.bfloat16).reshape(
        local_experts, owner_count, item_count, feat_width
    )
    returned = lax.all_to_all(expert_out, "expert", split_axis=1, concat_axis=1, tiled=True)
    flat_back = returned.reshape(slot_total, feat_width)
    picked = flat_back[jnp.minimum(slot_index, slot_total - 1)].reshape(
        row_count, route_count, feat_width
    )
    mixture = jnp.einsum("rk,rkd->rd", gate_weights, picked, preferred_element_type=jnp.float32)
    updated = widened + mixture
    dest_hot = (next_device[:, None] == jnp.arange(owner_count, dtype=jnp.int32)[None, :]).astype(
        jnp.int32
    ) * survive[:, None]
    dest_before = jnp.cumsum(dest_hot, axis=0) - dest_hot
    handoff_pos = jnp.sum(dest_before * dest_hot, axis=1)
    hand_slot = jnp.where(survive > 0, next_device * hand_cap + handoff_pos, owner_count * hand_cap)
    row_plus = jnp.arange(row_count, dtype=jnp.int32) + 1
    target = (
        jnp.zeros((owner_count * hand_cap,), jnp.int32).at[hand_slot].set(row_plus, mode="drop")
    )
    stacked = jnp.concatenate([jnp.zeros((1, feat_width), jnp.float32), updated], axis=0)
    leaving = stacked[target].reshape(owner_count, hand_cap, feat_width)
    arrived = lax.all_to_all(leaving, "expert", split_axis=0, concat_axis=0, tiled=True)
    return arrived.reshape(owner_count * hand_cap, feat_width)


def solution(mesh):
    in_specs = (
        P("expert", "rep"),
        P("rep"),
        P("expert", None),
        P("expert"),
        P("expert", None),
        P("expert"),
        P("expert", "rep", None),
        P("expert", None, "rep"),
    )
    out_specs = P("expert", "rep")
    return jax.shard_map(
        per_device, mesh=mesh, in_specs=in_specs, out_specs=out_specs, check_vma=False
    )
```

```python
import jax
import jax.numpy as jnp
from jax import lax
from jax.sharding import PartitionSpec as P


def per_device(
    tokens, norm_gain, gate_weights, exit_flags, routes, next_device, up_weight, down_weight
):
    row_count, feat_width = tokens.shape
    owner_count = lax.axis_size("expert")
    rep_count = lax.axis_size("rep")
    local_experts = up_weight.shape[0]
    hid = up_weight.shape[2]
    route_count = routes.shape[1]
    experts_all = local_experts * owner_count
    most_live = row_count // 2
    capacity = route_count * most_live // experts_all
    hand_cap = (most_live + owner_count - 1) // owner_count
    slot_total = local_experts * owner_count * capacity
    hid_part = hid // rep_count
    widened = tokens.astype(jnp.float32)
    survive = 1 - exit_flags
    pair_live = jnp.repeat(survive, route_count)
    route_flat = routes.reshape(-1)
    one_hot = (route_flat[:, None] == jnp.arange(experts_all, dtype=jnp.int32)[None, :]).astype(
        jnp.int32
    ) * pair_live[:, None]
    earlier = jnp.cumsum(one_hot, axis=0) - one_hot
    position = jnp.sum(earlier * one_hot, axis=1)
    owner_id = route_flat // local_experts
    local_id = route_flat % local_experts
    slot_index = (local_id * owner_count + owner_id) * capacity + position
    slot_index = jnp.where(pair_live > 0, slot_index, slot_total)
    squares = lax.psum(jnp.sum(widened * widened, axis=1), "rep")
    rinv_rows = lax.rsqrt(squares / (feat_width * rep_count) + 1e-06)
    normed = (widened * rinv_rows[:, None] * norm_gain[None, :]).astype(jnp.bfloat16)
    slot_ids = jnp.arange(slot_total, dtype=jnp.int32)
    slot_of = slot_index.reshape(row_count, route_count)
    pick = jnp.sum(
        (slot_of[None, :, :] == slot_ids[:, None, None]).astype(jnp.float32), axis=2
    ).astype(jnp.bfloat16)
    outbound = jnp.dot(pick, normed, preferred_element_type=jnp.float32).astype(jnp.bfloat16)
    outbound = outbound.reshape(local_experts, owner_count, capacity, feat_width)
    received = lax.all_to_all(outbound, "expert", split_axis=1, concat_axis=1, tiled=True)
    item_count = received.shape[2]
    rows_here = owner_count * item_count
    flattened = received.reshape(local_experts, rows_here, feat_width)
    partial_value = jnp.einsum(
        "erd,edh->erh", flattened, up_weight, preferred_element_type=jnp.float32
    )
    pieces = partial_value.reshape(local_experts * rows_here, rep_count, hid_part)
    pieces = jnp.transpose(pieces, (1, 0, 2))
    got = lax.all_to_all(pieces, "rep", split_axis=0, concat_axis=0, tiled=True)
    hidden_part = jnp.sum(got, axis=0).reshape(local_experts, rows_here, hid_part)
    act_part = jax.nn.silu(hidden_part).astype(jnp.bfloat16)
    act_tile = jnp.broadcast_to(act_part[None], (rep_count,) + act_part.shape)
    act_all = lax.all_to_all(act_tile, "rep", split_axis=0, concat_axis=0, tiled=True)
    activated = jnp.transpose(act_all, (1, 2, 0, 3)).reshape(local_experts, rows_here, hid)
    expert_out = jnp.einsum(
        "erh,ehd->erd", activated, down_weight, preferred_element_type=jnp.float32
    )
    expert_out = expert_out.astype(jnp.bfloat16).reshape(
        local_experts, owner_count, item_count, feat_width
    )
    returned = lax.all_to_all(expert_out, "expert", split_axis=1, concat_axis=1, tiled=True)
    flat_back = returned.reshape(slot_total, feat_width)
    combine = jnp.sum(
        jnp.where(
            slot_of[:, :, None] == slot_ids[None, None, :], gate_weights[:, :, None], 0.0
        ),
        axis=1,
    )
    mixture = jnp.dot(
        combine,
        flat_back.astype(jnp.float32),
        precision=lax.Precision.HIGHEST,
        preferred_element_type=jnp.float32,
    )
    updated = widened + mixture
    dest_hot = (next_device[:, None] == jnp.arange(owner_count, dtype=jnp.int32)[None, :]).astype(
        jnp.int32
    ) * survive[:, None]
    dest_before = jnp.cumsum(dest_hot, axis=0) - dest_hot
    handoff_pos = jnp.sum(dest_before * dest_hot, axis=1)
    hand_slot = jnp.where(survive > 0, next_device * hand_cap + handoff_pos, owner_count * hand_cap)
    row_plus = jnp.arange(row_count, dtype=jnp.int32) + 1
    target = (
        jnp.zeros((owner_count * hand_cap,), jnp.int32).at[hand_slot].set(row_plus, mode="drop")
    )
    stacked = jnp.concatenate([jnp.zeros((1, feat_width), jnp.float32), updated], axis=0)
    leaving = stacked[target].reshape(owner_count, hand_cap, feat_width)
    arrived = lax.all_to_all(leaving, "expert", split_axis=0, concat_axis=0, tiled=True)
    return arrived.reshape(owner_count * hand_cap, feat_width)


def solution(mesh):
    in_specs = (
        P("expert", "rep"),
        P("rep"),
        P("expert", None),
        P("expert"),
        P("expert", None),
        P("expert"),
        P("expert", "rep", None),
        P("expert", None, "rep"),
    )
    out_specs = P("expert", "rep")
    return jax.shard_map(
        per_device, mesh=mesh, in_specs=in_specs, out_specs=out_specs, check_vma=False
    )
```

```python
import jax
import jax.numpy as jnp
from jax import lax
from jax.sharding import Mesh, PartitionSpec as P


def per_device(
    tokens, norm_gain, gate_weights, exit_flags, routes, next_device, up_weight, down_weight
):
    row_count, feat_width = tokens.shape
    owner_count = lax.axis_size("expert")
    rep_count = lax.axis_size("ry") * lax.axis_size("rc")
    local_experts = up_weight.shape[0]
    hid = up_weight.shape[2]
    route_count = routes.shape[1]
    experts_all = local_experts * owner_count
    most_live = row_count // 2
    capacity = route_count * most_live // experts_all
    hand_cap = (most_live + owner_count - 1) // owner_count
    slot_total = local_experts * owner_count * capacity
    hid_part = hid // rep_count
    widened = tokens.astype(jnp.float32)
    survive = 1 - exit_flags
    pair_live = jnp.repeat(survive, route_count)
    route_flat = routes.reshape(-1)
    one_hot = (route_flat[:, None] == jnp.arange(experts_all, dtype=jnp.int32)[None, :]).astype(
        jnp.int32
    ) * pair_live[:, None]
    earlier = jnp.cumsum(one_hot, axis=0) - one_hot
    position = jnp.sum(earlier * one_hot, axis=1)
    owner_id = route_flat // local_experts
    local_id = route_flat % local_experts
    slot_index = (local_id * owner_count + owner_id) * capacity + position
    slot_index = jnp.where(pair_live > 0, slot_index, slot_total)
    squares = lax.psum(jnp.sum(widened * widened, axis=1), ("ry", "rc"))
    rinv_rows = lax.rsqrt(squares / (feat_width * rep_count) + 1e-06)
    normed = (widened * rinv_rows[:, None] * norm_gain[None, :]).astype(jnp.bfloat16)
    slot_ids = jnp.arange(slot_total, dtype=jnp.int32)
    slot_of = slot_index.reshape(row_count, route_count)
    pick = jnp.sum(
        (slot_of[None, :, :] == slot_ids[:, None, None]).astype(jnp.float32), axis=2
    ).astype(jnp.bfloat16)
    outbound = jnp.dot(pick, normed, preferred_element_type=jnp.float32).astype(jnp.bfloat16)
    outbound = outbound.reshape(local_experts, owner_count, capacity, feat_width)
    received = lax.all_to_all(outbound, "expert", split_axis=1, concat_axis=1, tiled=True)
    item_count = received.shape[2]
    rows_here = owner_count * item_count
    flattened = received.reshape(local_experts, rows_here, feat_width)
    partial_value = jnp.einsum(
        "erd,edh->erh", flattened, up_weight, preferred_element_type=jnp.float32
    )
    core = lax.axis_index("rc")
    sibling = [(i, 1 - i) for i in range(2)]
    chips = lax.axis_size("ry")
    half = hid // 2
    quarter = half // chips
    halves = partial_value.reshape(local_experts, rows_here, 2, half)
    mine = jnp.where(core == 0, halves[:, :, 0], halves[:, :, 1])
    theirs = jnp.where(core == 0, halves[:, :, 1], halves[:, :, 0])
    half_sum = mine + lax.ppermute(theirs, "rc", sibling)
    pieces = half_sum.reshape(local_experts * rows_here, chips, quarter)
    pieces = jnp.transpose(pieces, (1, 0, 2))
    got = lax.all_to_all(pieces, "ry", split_axis=0, concat_axis=0, tiled=True)
    hidden_part = jnp.sum(got, axis=0).reshape(local_experts, rows_here, quarter)
    act_part = jax.nn.silu(hidden_part).astype(jnp.bfloat16)
    act_tile = jnp.broadcast_to(act_part[None], (chips,) + act_part.shape)
    act_got = lax.all_to_all(act_tile, "ry", split_axis=0, concat_axis=0, tiled=True)
    act_half = jnp.transpose(act_got, (1, 2, 0, 3)).reshape(local_experts, rows_here, half)
    act_other = lax.ppermute(act_half, "rc", sibling)
    activated = jnp.where(
        core == 0,
        jnp.concatenate([act_half, act_other], axis=2),
        jnp.concatenate([act_other, act_half], axis=2),
    )
    expert_out = jnp.einsum(
        "erh,ehd->erd", activated, down_weight, preferred_element_type=jnp.float32
    )
    expert_out = expert_out.astype(jnp.bfloat16).reshape(
        local_experts, owner_count, item_count, feat_width
    )
    returned = lax.all_to_all(expert_out, "expert", split_axis=1, concat_axis=1, tiled=True)
    flat_back = returned.reshape(slot_total, feat_width)
    combine = jnp.sum(
        jnp.where(
            slot_of[:, :, None] == slot_ids[None, None, :], gate_weights[:, :, None], 0.0
        ),
        axis=1,
    )
    mixture = jnp.dot(
        combine,
        flat_back.astype(jnp.float32),
        precision=lax.Precision.HIGHEST,
        preferred_element_type=jnp.float32,
    )
    updated = widened + mixture
    dest_hot = (next_device[:, None] == jnp.arange(owner_count, dtype=jnp.int32)[None, :]).astype(
        jnp.int32
    ) * survive[:, None]
    dest_before = jnp.cumsum(dest_hot, axis=0) - dest_hot
    handoff_pos = jnp.sum(dest_before * dest_hot, axis=1)
    hand_slot = jnp.where(survive > 0, next_device * hand_cap + handoff_pos, owner_count * hand_cap)
    row_plus = jnp.arange(row_count, dtype=jnp.int32) + 1
    target = (
        jnp.zeros((owner_count * hand_cap,), jnp.int32).at[hand_slot].set(row_plus, mode="drop")
    )
    stacked = jnp.concatenate([jnp.zeros((1, feat_width), jnp.float32), updated], axis=0)
    leaving = stacked[target].reshape(owner_count, hand_cap, feat_width)
    arrived = lax.all_to_all(leaving, "expert", split_axis=0, concat_axis=0, tiled=True)
    return arrived.reshape(owner_count * hand_cap, feat_width)


def solution(mesh):
    chips = mesh.shape["rep"] // 2
    split = Mesh(
        mesh.devices.reshape(chips, 2, mesh.shape["expert"]), ("ry", "rc", "expert")
    )
    rep = ("ry", "rc")
    in_specs = (
        P("expert", rep),
        P(rep),
        P("expert", None),
        P("expert"),
        P("expert", None),
        P("expert"),
        P("expert", rep, None),
        P("expert", None, rep),
    )
    out_specs = P("expert", rep)
    return jax.shard_map(
        per_device, mesh=split, in_specs=in_specs, out_specs=out_specs, check_vma=False
    )
```

```python
import jax
import jax.numpy as jnp
from jax import lax
from jax.sharding import Mesh, PartitionSpec as P


def per_device(
    tokens, norm_gain, gate_weights, exit_flags, routes, next_device, up_weight, down_weight
):
    row_count, feat_width = tokens.shape
    owner_count = lax.axis_size("expert")
    rep_count = lax.axis_size("ry") * lax.axis_size("rc")
    local_experts = up_weight.shape[0]
    hid = up_weight.shape[2]
    route_count = routes.shape[1]
    experts_all = local_experts * owner_count
    most_live = row_count // 2
    capacity = route_count * most_live // experts_all
    hand_cap = (most_live + owner_count - 1) // owner_count
    slot_total = local_experts * owner_count * capacity
    hid_part = hid // rep_count
    widened = tokens.astype(jnp.float32)
    survive = 1 - exit_flags
    pair_live = jnp.repeat(survive, route_count)
    route_flat = routes.reshape(-1)
    one_hot = (route_flat[:, None] == jnp.arange(experts_all, dtype=jnp.int32)[None, :]).astype(
        jnp.int32
    ) * pair_live[:, None]
    earlier = jnp.cumsum(one_hot, axis=0) - one_hot
    position = jnp.sum(earlier * one_hot, axis=1)
    owner_id = route_flat // local_experts
    local_id = route_flat % local_experts
    slot_index = (local_id * owner_count + owner_id) * capacity + position
    slot_index = jnp.where(pair_live > 0, slot_index, slot_total)
    squares = lax.psum(jnp.sum(widened * widened, axis=1), ("ry", "rc"))
    rinv_rows = lax.rsqrt(squares / (feat_width * rep_count) + 1e-06)
    normed = (widened * rinv_rows[:, None] * norm_gain[None, :]).astype(jnp.bfloat16)
    slot_ids = jnp.arange(slot_total, dtype=jnp.int32)
    slot_of = slot_index.reshape(row_count, route_count)
    pick = jnp.sum(
        (slot_of[None, :, :] == slot_ids[:, None, None]).astype(jnp.float32), axis=2
    ).astype(jnp.bfloat16)
    outbound = jnp.dot(pick, normed, preferred_element_type=jnp.float32).astype(jnp.bfloat16)
    outbound = outbound.reshape(local_experts, owner_count, capacity, feat_width)
    received = lax.all_to_all(outbound, "expert", split_axis=1, concat_axis=1, tiled=True)
    item_count = received.shape[2]
    rows_here = owner_count * item_count
    flattened = received.reshape(local_experts, rows_here, feat_width)
    partial_value = jnp.einsum(
        "erd,edh->erh", flattened, up_weight, preferred_element_type=jnp.float32
    )
    core = lax.axis_index("rc")
    sibling = [(i, 1 - i) for i in range(2)]
    chips = lax.axis_size("ry")
    quarter = hid // (2 * chips)
    pieces = partial_value.reshape(local_experts * rows_here, 2 * chips, quarter)
    pieces = jnp.transpose(pieces, (1, 0, 2)).reshape(2, chips, local_experts * rows_here, quarter)
    mine = lax.dynamic_index_in_dim(pieces, core, axis=0, keepdims=False)
    theirs = lax.dynamic_index_in_dim(pieces, 1 - core, axis=0, keepdims=False)
    half_sum = mine + lax.ppermute(theirs, "rc", sibling)
    got = lax.all_to_all(half_sum, "ry", split_axis=0, concat_axis=0, tiled=True)
    hidden_part = jnp.sum(got, axis=0)
    act_part = jax.nn.silu(hidden_part).astype(jnp.bfloat16)
    act_tile = jnp.broadcast_to(act_part[None], (chips,) + act_part.shape)
    act_half = lax.all_to_all(act_tile, "ry", split_axis=0, concat_axis=0, tiled=True)
    act_other = lax.ppermute(act_half, "rc", sibling)
    down_q = down_weight.reshape(local_experts, 2, chips, quarter, feat_width)
    down_mine = lax.dynamic_index_in_dim(down_q, core, axis=1, keepdims=False)
    down_other = lax.dynamic_index_in_dim(down_q, 1 - core, axis=1, keepdims=False)
    act_half = act_half.reshape(chips, local_experts, rows_here, quarter)
    act_other = act_other.reshape(chips, local_experts, rows_here, quarter)
    expert_out = jnp.einsum(
        "qerj,eqjd->erd", act_half, down_mine, preferred_element_type=jnp.float32
    ) + jnp.einsum("qerj,eqjd->erd", act_other, down_other, preferred_element_type=jnp.float32)
    expert_out = expert_out.astype(jnp.bfloat16).reshape(
        local_experts, owner_count, item_count, feat_width
    )
    returned = lax.all_to_all(expert_out, "expert", split_axis=1, concat_axis=1, tiled=True)
    flat_back = returned.reshape(slot_total, feat_width)
    combine = jnp.sum(
        jnp.where(
            slot_of[:, :, None] == slot_ids[None, None, :], gate_weights[:, :, None], 0.0
        ),
        axis=1,
    )
    mixture = jnp.dot(
        combine,
        flat_back.astype(jnp.float32),
        precision=lax.Precision.HIGHEST,
        preferred_element_type=jnp.float32,
    )
    updated = widened + mixture
    dest_hot = (next_device[:, None] == jnp.arange(owner_count, dtype=jnp.int32)[None, :]).astype(
        jnp.int32
    ) * survive[:, None]
    dest_before = jnp.cumsum(dest_hot, axis=0) - dest_hot
    handoff_pos = jnp.sum(dest_before * dest_hot, axis=1)
    hand_slot = jnp.where(survive > 0, next_device * hand_cap + handoff_pos, owner_count * hand_cap)
    row_plus = jnp.arange(row_count, dtype=jnp.int32) + 1
    target = (
        jnp.zeros((owner_count * hand_cap,), jnp.int32).at[hand_slot].set(row_plus, mode="drop")
    )
    stacked = jnp.concatenate([jnp.zeros((1, feat_width), jnp.float32), updated], axis=0)
    leaving = stacked[target].reshape(owner_count, hand_cap, feat_width)
    arrived = lax.all_to_all(leaving, "expert", split_axis=0, concat_axis=0, tiled=True)
    return arrived.reshape(owner_count * hand_cap, feat_width)


def solution(mesh):
    chips = mesh.shape["rep"] // 2
    split = Mesh(
        mesh.devices.reshape(chips, 2, mesh.shape["expert"]), ("ry", "rc", "expert")
    )
    rep = ("ry", "rc")
    in_specs = (
        P("expert", rep),
        P(rep),
        P("expert", None),
        P("expert"),
        P("expert", None),
        P("expert"),
        P("expert", rep, None),
        P("expert", None, rep),
    )
    out_specs = P("expert", rep)
    return jax.shard_map(
        per_device, mesh=split, in_specs=in_specs, out_specs=out_specs, check_vma=False
    )
```

```python
import jax
import jax.numpy as jnp
from jax import lax
from jax.sharding import Mesh, PartitionSpec as P


def per_device(
    tokens, norm_gain, gate_weights, exit_flags, routes, next_device, up_weight, down_weight
):
    row_count, feat_width = tokens.shape
    owner_count = lax.axis_size("expert")
    rep_count = lax.axis_size("ry") * lax.axis_size("rc")
    local_experts = up_weight.shape[0]
    hid = up_weight.shape[2]
    route_count = routes.shape[1]
    experts_all = local_experts * owner_count
    most_live = row_count // 2
    capacity = route_count * most_live // experts_all
    hand_cap = (most_live + owner_count - 1) // owner_count
    slot_total = local_experts * owner_count * capacity
    hid_part = hid // rep_count
    widened = tokens.astype(jnp.float32)
    survive = 1 - exit_flags
    pair_live = jnp.repeat(survive, route_count)
    route_flat = routes.reshape(-1)
    one_hot = (route_flat[:, None] == jnp.arange(experts_all, dtype=jnp.int32)[None, :]).astype(
        jnp.int32
    ) * pair_live[:, None]
    earlier = jnp.cumsum(one_hot, axis=0) - one_hot
    position = jnp.sum(earlier * one_hot, axis=1)
    owner_id = route_flat // local_experts
    local_id = route_flat % local_experts
    slot_index = (local_id * owner_count + owner_id) * capacity + position
    slot_index = jnp.where(pair_live > 0, slot_index, slot_total)
    squares = jnp.sum(widened * widened, axis=1)
    chip = lax.axis_index("ry")
    chips = lax.axis_size("ry")
    for axis, bit in (("rc", 1), ("ry", 1), ("ry", 2)):
        pairs = [(i, i ^ bit) for i in range(lax.axis_size(axis))]
        squares = squares + lax.ppermute(squares, axis, pairs)
    rinv_rows = lax.rsqrt(squares / (feat_width * rep_count) + 1e-06)
    normed = (widened * rinv_rows[:, None] * norm_gain[None, :]).astype(jnp.bfloat16)
    slot_ids = jnp.arange(slot_total, dtype=jnp.int32)
    slot_of = slot_index.reshape(row_count, route_count)
    pick = jnp.sum(
        (slot_of[None, :, :] == slot_ids[:, None, None]).astype(jnp.float32), axis=2
    ).astype(jnp.bfloat16)
    outbound = jnp.dot(pick, normed, preferred_element_type=jnp.float32).astype(jnp.bfloat16)
    outbound = outbound.reshape(local_experts, owner_count, capacity, feat_width)
    received = lax.all_to_all(outbound, "expert", split_axis=1, concat_axis=1, tiled=True)
    item_count = received.shape[2]
    rows_here = owner_count * item_count
    flattened = received.reshape(local_experts, rows_here, feat_width)
    partial_value = jnp.einsum(
        "erd,edh->erh", flattened, up_weight, preferred_element_type=jnp.float32
    )
    core = lax.axis_index("rc")
    sibling = [(i, 1 - i) for i in range(2)]
    quarter = hid // (2 * chips)
    pieces = partial_value.reshape(local_experts * rows_here, 2 * chips, quarter)
    pieces = jnp.transpose(pieces, (1, 0, 2)).reshape(2, chips, local_experts * rows_here, quarter)
    mine = lax.dynamic_index_in_dim(pieces, core, axis=0, keepdims=False)
    theirs = lax.dynamic_index_in_dim(pieces, 1 - core, axis=0, keepdims=False)
    half_sum = mine + lax.ppermute(theirs, "rc", sibling)
    by_bit = half_sum.reshape(2, 2, local_experts * rows_here, quarter)
    low_bit, high_bit = chip % 2, chip // 2
    keep = lax.dynamic_index_in_dim(by_bit, low_bit, axis=1, keepdims=False)
    give = lax.dynamic_index_in_dim(by_bit, 1 - low_bit, axis=1, keepdims=False)
    keep = keep + lax.ppermute(give, "ry", [(i, i ^ 1) for i in range(chips)])
    give = lax.dynamic_index_in_dim(keep, 1 - high_bit, axis=0, keepdims=False)
    keep = lax.dynamic_index_in_dim(keep, high_bit, axis=0, keepdims=False)
    hidden_part = keep + lax.ppermute(give, "ry", [(i, i ^ 2) for i in range(chips)])
    act_part = jax.nn.silu(hidden_part).astype(jnp.bfloat16)
    act_two = jnp.stack(
        [act_part, lax.ppermute(act_part, "ry", [(i, i ^ 2) for i in range(chips)])]
    )
    act_half = jnp.concatenate(
        [act_two, lax.ppermute(act_two, "ry", [(i, i ^ 1) for i in range(chips)])]
    )
    order = jnp.array([0, 2, 1, 3], jnp.int32)
    act_other = lax.ppermute(act_half, "rc", sibling)
    down_q = down_weight.reshape(local_experts, 2, chips, quarter, feat_width)
    down_mine = jnp.take(
        lax.dynamic_index_in_dim(down_q, core, axis=1, keepdims=False), chip ^ order, axis=1
    )
    down_other = jnp.take(
        lax.dynamic_index_in_dim(down_q, 1 - core, axis=1, keepdims=False), chip ^ order, axis=1
    )
    act_half = act_half.reshape(chips, local_experts, rows_here, quarter)
    act_other = act_other.reshape(chips, local_experts, rows_here, quarter)
    expert_out = jnp.einsum(
        "qerj,eqjd->erd", act_half, down_mine, preferred_element_type=jnp.float32
    ) + jnp.einsum("qerj,eqjd->erd", act_other, down_other, preferred_element_type=jnp.float32)
    expert_out = expert_out.astype(jnp.bfloat16).reshape(
        local_experts, owner_count, item_count, feat_width
    )
    returned = lax.all_to_all(expert_out, "expert", split_axis=1, concat_axis=1, tiled=True)
    flat_back = returned.reshape(slot_total, feat_width)
    combine = jnp.sum(
        jnp.where(
            slot_of[:, :, None] == slot_ids[None, None, :], gate_weights[:, :, None], 0.0
        ),
        axis=1,
    )
    mixture = jnp.dot(
        combine,
        flat_back.astype(jnp.float32),
        precision=lax.Precision.HIGHEST,
        preferred_element_type=jnp.float32,
    )
    updated = widened + mixture
    dest_hot = (next_device[:, None] == jnp.arange(owner_count, dtype=jnp.int32)[None, :]).astype(
        jnp.int32
    ) * survive[:, None]
    dest_before = jnp.cumsum(dest_hot, axis=0) - dest_hot
    handoff_pos = jnp.sum(dest_before * dest_hot, axis=1)
    hand_slot = jnp.where(survive > 0, next_device * hand_cap + handoff_pos, owner_count * hand_cap)
    row_plus = jnp.arange(row_count, dtype=jnp.int32) + 1
    target = (
        jnp.zeros((owner_count * hand_cap,), jnp.int32).at[hand_slot].set(row_plus, mode="drop")
    )
    stacked = jnp.concatenate([jnp.zeros((1, feat_width), jnp.float32), updated], axis=0)
    leaving = stacked[target].reshape(owner_count, hand_cap, feat_width)
    arrived = lax.all_to_all(leaving, "expert", split_axis=0, concat_axis=0, tiled=True)
    return arrived.reshape(owner_count * hand_cap, feat_width)


def solution(mesh):
    chips = mesh.shape["rep"] // 2
    split = Mesh(
        mesh.devices.reshape(chips, 2, mesh.shape["expert"]), ("ry", "rc", "expert")
    )
    rep = ("ry", "rc")
    in_specs = (
        P("expert", rep),
        P(rep),
        P("expert", None),
        P("expert"),
        P("expert", None),
        P("expert"),
        P("expert", rep, None),
        P("expert", None, rep),
    )
    out_specs = P("expert", rep)
    return jax.shard_map(
        per_device, mesh=split, in_specs=in_specs, out_specs=out_specs, check_vma=False
    )
```

```python
import jax
import jax.numpy as jnp
from jax import lax
from jax.sharding import Mesh, PartitionSpec as P


def per_device(
    tokens, norm_gain, gate_weights, exit_flags, routes, next_device, up_weight, down_weight
):
    row_count, feat_width = tokens.shape
    owner_count = lax.axis_size("expert")
    rep_count = lax.axis_size("ry") * lax.axis_size("rc")
    local_experts = up_weight.shape[0]
    hid = up_weight.shape[2]
    route_count = routes.shape[1]
    experts_all = local_experts * owner_count
    most_live = row_count // 2
    capacity = route_count * most_live // experts_all
    hand_cap = (most_live + owner_count - 1) // owner_count
    slot_total = local_experts * owner_count * capacity
    hid_part = hid // rep_count
    widened = tokens.astype(jnp.float32)
    survive = 1 - exit_flags
    pair_live = jnp.repeat(survive, route_count)
    route_flat = routes.reshape(-1)
    one_hot = (route_flat[:, None] == jnp.arange(experts_all, dtype=jnp.int32)[None, :]).astype(
        jnp.int32
    ) * pair_live[:, None]
    earlier = jnp.cumsum(one_hot, axis=0) - one_hot
    position = jnp.sum(earlier * one_hot, axis=1)
    owner_id = route_flat // local_experts
    local_id = route_flat % local_experts
    slot_index = (local_id * owner_count + owner_id) * capacity + position
    slot_index = jnp.where(pair_live > 0, slot_index, slot_total)
    squares = jnp.sum(widened * widened, axis=1)
    squares = squares + lax.ppermute(squares, "rc", [(0, 1), (1, 0)])
    squares = lax.psum(squares, "ry")
    rinv_rows = lax.rsqrt(squares / (feat_width * rep_count) + 1e-06)
    normed = (widened * rinv_rows[:, None] * norm_gain[None, :]).astype(jnp.bfloat16)
    slot_ids = jnp.arange(slot_total, dtype=jnp.int32)
    slot_of = slot_index.reshape(row_count, route_count)
    pick = jnp.sum(
        (slot_of[None, :, :] == slot_ids[:, None, None]).astype(jnp.float32), axis=2
    ).astype(jnp.bfloat16)
    outbound = jnp.dot(pick, normed, preferred_element_type=jnp.float32).astype(jnp.bfloat16)
    outbound = outbound.reshape(local_experts, owner_count, capacity, feat_width)
    received = lax.all_to_all(outbound, "expert", split_axis=1, concat_axis=1, tiled=True)
    item_count = received.shape[2]
    rows_here = owner_count * item_count
    flattened = received.reshape(local_experts, rows_here, feat_width)
    partial_value = jnp.einsum(
        "erd,edh->erh", flattened, up_weight, preferred_element_type=jnp.float32
    )
    core = lax.axis_index("rc")
    sibling = [(i, 1 - i) for i in range(2)]
    chips = lax.axis_size("ry")
    quarter = hid // (2 * chips)
    pieces = partial_value.reshape(local_experts * rows_here, 2 * chips, quarter)
    pieces = jnp.transpose(pieces, (1, 0, 2)).reshape(2, chips, local_experts * rows_here, quarter)
    mine = lax.dynamic_index_in_dim(pieces, core, axis=0, keepdims=False)
    theirs = lax.dynamic_index_in_dim(pieces, 1 - core, axis=0, keepdims=False)
    half_sum = mine + lax.ppermute(theirs, "rc", sibling)
    got = lax.all_to_all(half_sum, "ry", split_axis=0, concat_axis=0, tiled=True)
    hidden_part = jnp.sum(got, axis=0)
    act_part = jax.nn.silu(hidden_part).astype(jnp.bfloat16)
    act_tile = jnp.broadcast_to(act_part[None], (chips,) + act_part.shape)
    act_half = lax.all_to_all(act_tile, "ry", split_axis=0, concat_axis=0, tiled=True)
    act_other = lax.ppermute(act_half, "rc", sibling)
    down_q = down_weight.reshape(local_experts, 2, chips, quarter, feat_width)
    down_mine = lax.dynamic_index_in_dim(down_q, core, axis=1, keepdims=False)
    down_other = lax.dynamic_index_in_dim(down_q, 1 - core, axis=1, keepdims=False)
    act_half = act_half.reshape(chips, local_experts, rows_here, quarter)
    act_other = act_other.reshape(chips, local_experts, rows_here, quarter)
    expert_out = jnp.einsum(
        "qerj,eqjd->erd", act_half, down_mine, preferred_element_type=jnp.float32
    ) + jnp.einsum("qerj,eqjd->erd", act_other, down_other, preferred_element_type=jnp.float32)
    expert_out = expert_out.astype(jnp.bfloat16).reshape(
        local_experts, owner_count, item_count, feat_width
    )
    returned = lax.all_to_all(expert_out, "expert", split_axis=1, concat_axis=1, tiled=True)
    flat_back = returned.reshape(slot_total, feat_width)
    combine = jnp.sum(
        jnp.where(
            slot_of[:, :, None] == slot_ids[None, None, :], gate_weights[:, :, None], 0.0
        ),
        axis=1,
    )
    mixture = jnp.dot(
        combine,
        flat_back.astype(jnp.float32),
        precision=lax.Precision.HIGHEST,
        preferred_element_type=jnp.float32,
    )
    updated = widened + mixture
    dest_hot = (next_device[:, None] == jnp.arange(owner_count, dtype=jnp.int32)[None, :]).astype(
        jnp.int32
    ) * survive[:, None]
    dest_before = jnp.cumsum(dest_hot, axis=0) - dest_hot
    handoff_pos = jnp.sum(dest_before * dest_hot, axis=1)
    hand_slot = jnp.where(survive > 0, next_device * hand_cap + handoff_pos, owner_count * hand_cap)
    row_plus = jnp.arange(row_count, dtype=jnp.int32) + 1
    target = (
        jnp.zeros((owner_count * hand_cap,), jnp.int32).at[hand_slot].set(row_plus, mode="drop")
    )
    stacked = jnp.concatenate([jnp.zeros((1, feat_width), jnp.float32), updated], axis=0)
    leaving = stacked[target].reshape(owner_count, hand_cap, feat_width)
    arrived = lax.all_to_all(leaving, "expert", split_axis=0, concat_axis=0, tiled=True)
    return arrived.reshape(owner_count * hand_cap, feat_width)


def solution(mesh):
    chips = mesh.shape["rep"] // 2
    split = Mesh(
        mesh.devices.reshape(chips, 2, mesh.shape["expert"]), ("ry", "rc", "expert")
    )
    rep = ("ry", "rc")
    in_specs = (
        P("expert", rep),
        P(rep),
        P("expert", None),
        P("expert"),
        P("expert", None),
        P("expert"),
        P("expert", rep, None),
        P("expert", None, rep),
    )
    out_specs = P("expert", rep)
    return jax.shard_map(
        per_device, mesh=split, in_specs=in_specs, out_specs=out_specs, check_vma=False
    )
```

```python
import jax
import jax.numpy as jnp
from jax import lax
from jax.sharding import Mesh, PartitionSpec as P


def per_device(
    tokens, norm_gain, gate_weights, exit_flags, routes, next_device, up_weight, down_weight
):
    row_count, feat_width = tokens.shape
    owner_count = lax.axis_size("expert")
    rep_count = lax.axis_size("ry") * lax.axis_size("rc")
    local_experts = up_weight.shape[0]
    hid = up_weight.shape[2]
    route_count = routes.shape[1]
    experts_all = local_experts * owner_count
    most_live = row_count // 2
    capacity = route_count * most_live // experts_all
    hand_cap = (most_live + owner_count - 1) // owner_count
    slot_total = local_experts * owner_count * capacity
    hid_part = hid // rep_count
    widened = tokens.astype(jnp.float32)
    survive = 1 - exit_flags
    pair_live = jnp.repeat(survive, route_count)
    route_flat = routes.reshape(-1)
    one_hot = (route_flat[:, None] == jnp.arange(experts_all, dtype=jnp.int32)[None, :]).astype(
        jnp.int32
    ) * pair_live[:, None]
    earlier = jnp.cumsum(one_hot, axis=0) - one_hot
    position = jnp.sum(earlier * one_hot, axis=1)
    owner_id = route_flat // local_experts
    local_id = route_flat % local_experts
    slot_index = (owner_id * local_experts + local_id) * capacity + position
    slot_index = jnp.where(pair_live > 0, slot_index, slot_total)
    squares = jnp.sum(widened * widened, axis=1)
    squares = squares + lax.ppermute(squares, "rc", [(0, 1), (1, 0)])
    squares = lax.psum(squares, "ry")
    rinv_rows = lax.rsqrt(squares / (feat_width * rep_count) + 1e-06)
    normed = (widened * rinv_rows[:, None] * norm_gain[None, :]).astype(jnp.bfloat16)
    slot_ids = jnp.arange(slot_total, dtype=jnp.int32)
    slot_of = slot_index.reshape(row_count, route_count)
    pick = jnp.sum(
        (slot_of[None, :, :] == slot_ids[:, None, None]).astype(jnp.float32), axis=2
    ).astype(jnp.bfloat16)
    outbound = jnp.dot(pick, normed, preferred_element_type=jnp.float32).astype(jnp.bfloat16)
    outbound = outbound.reshape(owner_count, local_experts * capacity, feat_width)
    received = lax.all_to_all(outbound, "expert", split_axis=0, concat_axis=0, tiled=True)
    item_count = capacity
    rows_here = owner_count * item_count
    flattened = jnp.transpose(
        received.reshape(owner_count, local_experts, capacity, feat_width), (1, 0, 2, 3)
    ).reshape(local_experts, rows_here, feat_width)
    partial_value = jnp.einsum(
        "erd,edh->erh", flattened, up_weight, preferred_element_type=jnp.float32
    )
    core = lax.axis_index("rc")
    sibling = [(i, 1 - i) for i in range(2)]
    chips = lax.axis_size("ry")
    quarter = hid // (2 * chips)
    pieces = partial_value.reshape(local_experts * rows_here, 2 * chips, quarter)
    pieces = jnp.transpose(pieces, (1, 0, 2)).reshape(2, chips, local_experts * rows_here, quarter)
    mine = lax.dynamic_index_in_dim(pieces, core, axis=0, keepdims=False)
    theirs = lax.dynamic_index_in_dim(pieces, 1 - core, axis=0, keepdims=False)
    half_sum = mine + lax.ppermute(theirs, "rc", sibling)
    got = lax.all_to_all(half_sum, "ry", split_axis=0, concat_axis=0, tiled=True)
    hidden_part = jnp.sum(got, axis=0)
    act_part = jax.nn.silu(hidden_part).astype(jnp.bfloat16)
    act_tile = jnp.broadcast_to(act_part[None], (chips,) + act_part.shape)
    act_half = lax.all_to_all(act_tile, "ry", split_axis=0, concat_axis=0, tiled=True)
    act_other = lax.ppermute(act_half, "rc", sibling)
    down_q = down_weight.reshape(local_experts, 2, chips, quarter, feat_width)
    down_mine = lax.dynamic_index_in_dim(down_q, core, axis=1, keepdims=False)
    down_other = lax.dynamic_index_in_dim(down_q, 1 - core, axis=1, keepdims=False)
    act_half = act_half.reshape(chips, local_experts, rows_here, quarter)
    act_other = act_other.reshape(chips, local_experts, rows_here, quarter)
    expert_out = jnp.einsum(
        "qerj,eqjd->erd", act_half, down_mine, preferred_element_type=jnp.float32
    ) + jnp.einsum("qerj,eqjd->erd", act_other, down_other, preferred_element_type=jnp.float32)
    expert_out = expert_out.astype(jnp.bfloat16).reshape(
        local_experts, owner_count, item_count, feat_width
    )
    expert_out = jnp.transpose(expert_out, (1, 0, 2, 3)).reshape(
        owner_count, local_experts * item_count, feat_width
    )
    returned = lax.all_to_all(expert_out, "expert", split_axis=0, concat_axis=0, tiled=True)
    flat_back = returned.reshape(slot_total, feat_width)
    combine = jnp.sum(
        jnp.where(
            slot_of[:, :, None] == slot_ids[None, None, :], gate_weights[:, :, None], 0.0
        ),
        axis=1,
    )
    mixture = jnp.dot(
        combine,
        flat_back.astype(jnp.float32),
        precision=lax.Precision.HIGHEST,
        preferred_element_type=jnp.float32,
    )
    updated = widened + mixture
    dest_hot = (next_device[:, None] == jnp.arange(owner_count, dtype=jnp.int32)[None, :]).astype(
        jnp.int32
    ) * survive[:, None]
    dest_before = jnp.cumsum(dest_hot, axis=0) - dest_hot
    handoff_pos = jnp.sum(dest_before * dest_hot, axis=1)
    hand_slot = jnp.where(survive > 0, next_device * hand_cap + handoff_pos, owner_count * hand_cap)
    row_plus = jnp.arange(row_count, dtype=jnp.int32) + 1
    target = (
        jnp.zeros((owner_count * hand_cap,), jnp.int32).at[hand_slot].set(row_plus, mode="drop")
    )
    stacked = jnp.concatenate([jnp.zeros((1, feat_width), jnp.float32), updated], axis=0)
    leaving = stacked[target].reshape(owner_count, hand_cap, feat_width)
    arrived = lax.all_to_all(leaving, "expert", split_axis=0, concat_axis=0, tiled=True)
    return arrived.reshape(owner_count * hand_cap, feat_width)


def solution(mesh):
    chips = mesh.shape["rep"] // 2
    split = Mesh(
        mesh.devices.reshape(chips, 2, mesh.shape["expert"]), ("ry", "rc", "expert")
    )
    rep = ("ry", "rc")
    in_specs = (
        P("expert", rep),
        P(rep),
        P("expert", None),
        P("expert"),
        P("expert", None),
        P("expert"),
        P("expert", rep, None),
        P("expert", None, rep),
    )
    out_specs = P("expert", rep)
    return jax.shard_map(
        per_device, mesh=split, in_specs=in_specs, out_specs=out_specs, check_vma=False
    )
```

```python
import jax
import jax.numpy as jnp
from jax import lax
from jax.sharding import Mesh, PartitionSpec as P


def per_device(
    tokens, norm_gain, gate_weights, exit_flags, routes, next_device, up_weight, down_weight
):
    row_count, feat_width = tokens.shape
    owner_count = lax.axis_size("expert")
    rep_count = lax.axis_size("ry") * lax.axis_size("rc")
    local_experts = up_weight.shape[0]
    hid = up_weight.shape[2]
    route_count = routes.shape[1]
    experts_all = local_experts * owner_count
    most_live = row_count // 2
    capacity = route_count * most_live // experts_all
    hand_cap = (most_live + owner_count - 1) // owner_count
    slot_total = local_experts * owner_count * capacity
    hid_part = hid // rep_count
    widened = tokens.astype(jnp.float32)
    survive = 1 - exit_flags
    pair_live = jnp.repeat(survive, route_count)
    route_flat = routes.reshape(-1)
    one_hot = (route_flat[:, None] == jnp.arange(experts_all, dtype=jnp.int32)[None, :]).astype(
        jnp.int32
    ) * pair_live[:, None]
    earlier = jnp.cumsum(one_hot, axis=0) - one_hot
    position = jnp.sum(earlier * one_hot, axis=1)
    owner_id = route_flat // local_experts
    local_id = route_flat % local_experts
    slot_index = (local_id * owner_count + owner_id) * capacity + position
    slot_index = jnp.where(pair_live > 0, slot_index, slot_total)
    squares = jnp.sum(widened * widened, axis=1)
    squares = squares + lax.ppermute(squares, "rc", [(0, 1), (1, 0)])
    chip_count = lax.axis_size("ry")
    spread = jnp.broadcast_to(squares[None], (chip_count,) + squares.shape)
    squares = jnp.sum(lax.all_to_all(spread, "ry", 0, 0, tiled=True), axis=0)
    rinv_rows = lax.rsqrt(squares / (feat_width * rep_count) + 1e-06)
    normed = (widened * rinv_rows[:, None] * norm_gain[None, :]).astype(jnp.bfloat16)
    slot_ids = jnp.arange(slot_total, dtype=jnp.int32)
    slot_of = slot_index.reshape(row_count, route_count)
    pick = jnp.sum(
        (slot_of[None, :, :] == slot_ids[:, None, None]).astype(jnp.float32), axis=2
    ).astype(jnp.bfloat16)
    outbound = jnp.dot(pick, normed, preferred_element_type=jnp.float32).astype(jnp.bfloat16)
    outbound = outbound.reshape(local_experts, owner_count, capacity, feat_width)
    received = lax.all_to_all(outbound, "expert", split_axis=1, concat_axis=1, tiled=True)
    item_count = received.shape[2]
    rows_here = owner_count * item_count
    flattened = received.reshape(local_experts, rows_here, feat_width)
    partial_value = jnp.einsum(
        "erd,edh->erh", flattened, up_weight, preferred_element_type=jnp.float32
    )
    core = lax.axis_index("rc")
    sibling = [(i, 1 - i) for i in range(2)]
    chips = lax.axis_size("ry")
    quarter = hid // (2 * chips)
    pieces = partial_value.reshape(local_experts * rows_here, 2 * chips, quarter)
    pieces = jnp.transpose(pieces, (1, 0, 2)).reshape(2, chips, local_experts * rows_here, quarter)
    mine = lax.dynamic_index_in_dim(pieces, core, axis=0, keepdims=False)
    theirs = lax.dynamic_index_in_dim(pieces, 1 - core, axis=0, keepdims=False)
    half_sum = mine + lax.ppermute(theirs, "rc", sibling)
    got = lax.all_to_all(half_sum, "ry", split_axis=0, concat_axis=0, tiled=True)
    hidden_part = jnp.sum(got, axis=0)
    act_part = jax.nn.silu(hidden_part).astype(jnp.bfloat16)
    act_tile = jnp.broadcast_to(act_part[None], (chips,) + act_part.shape)
    act_half = lax.all_to_all(act_tile, "ry", split_axis=0, concat_axis=0, tiled=True)
    act_other = lax.ppermute(act_half, "rc", sibling)
    down_q = down_weight.reshape(local_experts, 2, chips, quarter, feat_width)
    down_mine = lax.dynamic_index_in_dim(down_q, core, axis=1, keepdims=False)
    down_other = lax.dynamic_index_in_dim(down_q, 1 - core, axis=1, keepdims=False)
    act_half = act_half.reshape(chips, local_experts, rows_here, quarter)
    act_other = act_other.reshape(chips, local_experts, rows_here, quarter)
    expert_out = jnp.einsum(
        "qerj,eqjd->erd", act_half, down_mine, preferred_element_type=jnp.float32
    ) + jnp.einsum("qerj,eqjd->erd", act_other, down_other, preferred_element_type=jnp.float32)
    expert_out = expert_out.astype(jnp.bfloat16).reshape(
        local_experts, owner_count, item_count, feat_width
    )
    returned = lax.all_to_all(expert_out, "expert", split_axis=1, concat_axis=1, tiled=True)
    flat_back = returned.reshape(slot_total, feat_width)
    combine = jnp.sum(
        jnp.where(
            slot_of[:, :, None] == slot_ids[None, None, :], gate_weights[:, :, None], 0.0
        ),
        axis=1,
    )
    mixture = jnp.dot(
        combine,
        flat_back.astype(jnp.float32),
        precision=lax.Precision.HIGHEST,
        preferred_element_type=jnp.float32,
    )
    updated = widened + mixture
    dest_hot = (next_device[:, None] == jnp.arange(owner_count, dtype=jnp.int32)[None, :]).astype(
        jnp.int32
    ) * survive[:, None]
    dest_before = jnp.cumsum(dest_hot, axis=0) - dest_hot
    handoff_pos = jnp.sum(dest_before * dest_hot, axis=1)
    hand_slot = jnp.where(survive > 0, next_device * hand_cap + handoff_pos, owner_count * hand_cap)
    row_plus = jnp.arange(row_count, dtype=jnp.int32) + 1
    target = (
        jnp.zeros((owner_count * hand_cap,), jnp.int32).at[hand_slot].set(row_plus, mode="drop")
    )
    stacked = jnp.concatenate([jnp.zeros((1, feat_width), jnp.float32), updated], axis=0)
    leaving = stacked[target].reshape(owner_count, hand_cap, feat_width)
    arrived = lax.all_to_all(leaving, "expert", split_axis=0, concat_axis=0, tiled=True)
    return arrived.reshape(owner_count * hand_cap, feat_width)


def solution(mesh):
    chips = mesh.shape["rep"] // 2
    split = Mesh(
        mesh.devices.reshape(chips, 2, mesh.shape["expert"]), ("ry", "rc", "expert")
    )
    rep = ("ry", "rc")
    in_specs = (
        P("expert", rep),
        P(rep),
        P("expert", None),
        P("expert"),
        P("expert", None),
        P("expert"),
        P("expert", rep, None),
        P("expert", None, rep),
    )
    out_specs = P("expert", rep)
    return jax.shard_map(
        per_device, mesh=split, in_specs=in_specs, out_specs=out_specs, check_vma=False
    )
```

```python
import jax
import jax.numpy as jnp
from jax import lax
from jax.sharding import Mesh, PartitionSpec as P


def per_device(
    tokens, norm_gain, gate_weights, exit_flags, routes, next_device, up_weight, down_weight
):
    row_count, feat_width = tokens.shape
    owner_count = lax.axis_size("expert")
    rep_count = lax.axis_size("ry") * lax.axis_size("rc")
    local_experts = up_weight.shape[0]
    hid = up_weight.shape[2]
    route_count = routes.shape[1]
    experts_all = local_experts * owner_count
    most_live = row_count // 2
    capacity = route_count * most_live // experts_all
    hand_cap = (most_live + owner_count - 1) // owner_count
    slot_total = local_experts * owner_count * capacity
    hid_part = hid // rep_count
    widened = tokens.astype(jnp.float32)
    survive = 1 - exit_flags
    pair_live = jnp.repeat(survive, route_count)
    route_flat = routes.reshape(-1)
    one_hot = (route_flat[:, None] == jnp.arange(experts_all, dtype=jnp.int32)[None, :]).astype(
        jnp.int32
    ) * pair_live[:, None]
    earlier = jnp.cumsum(one_hot, axis=0) - one_hot
    position = jnp.sum(earlier * one_hot, axis=1)
    owner_id = route_flat // local_experts
    local_id = route_flat % local_experts
    slot_index = (local_id * owner_count + owner_id) * capacity + position
    slot_index = jnp.where(pair_live > 0, slot_index, slot_total)
    squares = jnp.sum(widened * widened, axis=1)
    spread = jnp.broadcast_to(squares[None], (rep_count,) + squares.shape)
    squares = jnp.sum(lax.all_to_all(spread, ("ry", "rc"), 0, 0, tiled=True), axis=0)
    rinv_rows = lax.rsqrt(squares / (feat_width * rep_count) + 1e-06)
    normed = (widened * rinv_rows[:, None] * norm_gain[None, :]).astype(jnp.bfloat16)
    slot_ids = jnp.arange(slot_total, dtype=jnp.int32)
    slot_of = slot_index.reshape(row_count, route_count)
    pick = jnp.sum(
        (slot_of[None, :, :] == slot_ids[:, None, None]).astype(jnp.float32), axis=2
    ).astype(jnp.bfloat16)
    outbound = jnp.dot(pick, normed, preferred_element_type=jnp.float32).astype(jnp.bfloat16)
    outbound = outbound.reshape(local_experts, owner_count, capacity, feat_width)
    received = lax.all_to_all(outbound, "expert", split_axis=1, concat_axis=1, tiled=True)
    item_count = received.shape[2]
    rows_here = owner_count * item_count
    flattened = received.reshape(local_experts, rows_here, feat_width)
    partial_value = jnp.einsum(
        "erd,edh->erh", flattened, up_weight, preferred_element_type=jnp.float32
    )
    core = lax.axis_index("rc")
    sibling = [(i, 1 - i) for i in range(2)]
    chips = lax.axis_size("ry")
    quarter = hid // (2 * chips)
    pieces = partial_value.reshape(local_experts * rows_here, 2 * chips, quarter)
    pieces = jnp.transpose(pieces, (1, 0, 2)).reshape(2, chips, local_experts * rows_here, quarter)
    mine = lax.dynamic_index_in_dim(pieces, core, axis=0, keepdims=False)
    theirs = lax.dynamic_index_in_dim(pieces, 1 - core, axis=0, keepdims=False)
    half_sum = mine + lax.ppermute(theirs, "rc", sibling)
    got = lax.all_to_all(half_sum, "ry", split_axis=0, concat_axis=0, tiled=True)
    hidden_part = jnp.sum(got, axis=0)
    act_part = jax.nn.silu(hidden_part).astype(jnp.bfloat16)
    act_tile = jnp.broadcast_to(act_part[None], (chips,) + act_part.shape)
    act_half = lax.all_to_all(act_tile, "ry", split_axis=0, concat_axis=0, tiled=True)
    act_other = lax.ppermute(act_half, "rc", sibling)
    down_q = down_weight.reshape(local_experts, 2, chips, quarter, feat_width)
    down_mine = lax.dynamic_index_in_dim(down_q, core, axis=1, keepdims=False)
    down_other = lax.dynamic_index_in_dim(down_q, 1 - core, axis=1, keepdims=False)
    act_half = act_half.reshape(chips, local_experts, rows_here, quarter)
    act_other = act_other.reshape(chips, local_experts, rows_here, quarter)
    expert_out = jnp.einsum(
        "qerj,eqjd->erd", act_half, down_mine, preferred_element_type=jnp.float32
    ) + jnp.einsum("qerj,eqjd->erd", act_other, down_other, preferred_element_type=jnp.float32)
    expert_out = expert_out.astype(jnp.bfloat16).reshape(
        local_experts, owner_count, item_count, feat_width
    )
    returned = lax.all_to_all(expert_out, "expert", split_axis=1, concat_axis=1, tiled=True)
    flat_back = returned.reshape(slot_total, feat_width)
    combine = jnp.sum(
        jnp.where(
            slot_of[:, :, None] == slot_ids[None, None, :], gate_weights[:, :, None], 0.0
        ),
        axis=1,
    )
    mixture = jnp.dot(
        combine,
        flat_back.astype(jnp.float32),
        precision=lax.Precision.HIGHEST,
        preferred_element_type=jnp.float32,
    )
    updated = widened + mixture
    dest_hot = (next_device[:, None] == jnp.arange(owner_count, dtype=jnp.int32)[None, :]).astype(
        jnp.int32
    ) * survive[:, None]
    dest_before = jnp.cumsum(dest_hot, axis=0) - dest_hot
    handoff_pos = jnp.sum(dest_before * dest_hot, axis=1)
    hand_slot = jnp.where(survive > 0, next_device * hand_cap + handoff_pos, owner_count * hand_cap)
    row_plus = jnp.arange(row_count, dtype=jnp.int32) + 1
    target = (
        jnp.zeros((owner_count * hand_cap,), jnp.int32).at[hand_slot].set(row_plus, mode="drop")
    )
    stacked = jnp.concatenate([jnp.zeros((1, feat_width), jnp.float32), updated], axis=0)
    leaving = stacked[target].reshape(owner_count, hand_cap, feat_width)
    arrived = lax.all_to_all(leaving, "expert", split_axis=0, concat_axis=0, tiled=True)
    return arrived.reshape(owner_count * hand_cap, feat_width)


def solution(mesh):
    chips = mesh.shape["rep"] // 2
    split = Mesh(
        mesh.devices.reshape(chips, 2, mesh.shape["expert"]), ("ry", "rc", "expert")
    )
    rep = ("ry", "rc")
    in_specs = (
        P("expert", rep),
        P(rep),
        P("expert", None),
        P("expert"),
        P("expert", None),
        P("expert"),
        P("expert", rep, None),
        P("expert", None, rep),
    )
    out_specs = P("expert", rep)
    return jax.shard_map(
        per_device, mesh=split, in_specs=in_specs, out_specs=out_specs, check_vma=False
    )
```

```python
import jax
import jax.numpy as jnp
from jax import lax
from jax.sharding import Mesh, PartitionSpec as P


def per_device(
    tokens, norm_gain, gate_weights, exit_flags, routes, next_device, up_weight, down_weight
):
    row_count, feat_width = tokens.shape
    owner_count = lax.axis_size("expert")
    rep_count = lax.axis_size("ry") * lax.axis_size("rc")
    local_experts = up_weight.shape[0]
    hid = up_weight.shape[2]
    route_count = routes.shape[1]
    experts_all = local_experts * owner_count
    most_live = row_count // 2
    capacity = route_count * most_live // experts_all
    hand_cap = (most_live + owner_count - 1) // owner_count
    slot_total = local_experts * owner_count * capacity
    hid_part = hid // rep_count
    widened = tokens.astype(jnp.float32)
    survive = 1 - exit_flags
    pair_live = jnp.repeat(survive, route_count)
    route_flat = routes.reshape(-1)
    one_hot = (route_flat[:, None] == jnp.arange(experts_all, dtype=jnp.int32)[None, :]).astype(
        jnp.int32
    ) * pair_live[:, None]
    earlier = jnp.cumsum(one_hot, axis=0) - one_hot
    position = jnp.sum(earlier * one_hot, axis=1)
    owner_id = route_flat // local_experts
    local_id = route_flat % local_experts
    slot_index = (local_id * owner_count + owner_id) * capacity + position
    slot_index = jnp.where(pair_live > 0, slot_index, slot_total)
    squares = jnp.dot(
        widened * widened,
        jnp.ones((feat_width, rep_count), jnp.float32),
        precision=lax.Precision.HIGHEST,
        preferred_element_type=jnp.float32,
    )
    spread = jnp.transpose(squares)
    squares = jnp.sum(lax.all_to_all(spread, ("ry", "rc"), 0, 0, tiled=True), axis=0)
    rinv_rows = lax.rsqrt(squares / (feat_width * rep_count) + 1e-06)
    normed = (widened * rinv_rows[:, None] * norm_gain[None, :]).astype(jnp.bfloat16)
    slot_ids = jnp.arange(slot_total, dtype=jnp.int32)
    slot_of = slot_index.reshape(row_count, route_count)
    pick = jnp.sum(
        (slot_of[None, :, :] == slot_ids[:, None, None]).astype(jnp.float32), axis=2
    ).astype(jnp.bfloat16)
    outbound = jnp.dot(pick, normed, preferred_element_type=jnp.float32).astype(jnp.bfloat16)
    outbound = outbound.reshape(local_experts, owner_count, capacity, feat_width)
    received = lax.all_to_all(outbound, "expert", split_axis=1, concat_axis=1, tiled=True)
    item_count = received.shape[2]
    rows_here = owner_count * item_count
    flattened = received.reshape(local_experts, rows_here, feat_width)
    partial_value = jnp.einsum(
        "erd,edh->erh", flattened, up_weight, preferred_element_type=jnp.float32
    )
    core = lax.axis_index("rc")
    sibling = [(i, 1 - i) for i in range(2)]
    chips = lax.axis_size("ry")
    quarter = hid // (2 * chips)
    pieces = partial_value.reshape(local_experts * rows_here, 2 * chips, quarter)
    pieces = jnp.transpose(pieces, (1, 0, 2)).reshape(2, chips, local_experts * rows_here, quarter)
    mine = lax.dynamic_index_in_dim(pieces, core, axis=0, keepdims=False)
    theirs = lax.dynamic_index_in_dim(pieces, 1 - core, axis=0, keepdims=False)
    half_sum = mine + lax.ppermute(theirs, "rc", sibling)
    got = lax.all_to_all(half_sum, "ry", split_axis=0, concat_axis=0, tiled=True)
    hidden_part = jnp.sum(got, axis=0)
    act_part = jax.nn.silu(hidden_part).astype(jnp.bfloat16)
    act_tile = jnp.broadcast_to(act_part[None], (chips,) + act_part.shape)
    act_half = lax.all_to_all(act_tile, "ry", split_axis=0, concat_axis=0, tiled=True)
    act_other = lax.ppermute(act_half, "rc", sibling)
    down_q = down_weight.reshape(local_experts, 2, chips, quarter, feat_width)
    down_mine = lax.dynamic_index_in_dim(down_q, core, axis=1, keepdims=False)
    down_other = lax.dynamic_index_in_dim(down_q, 1 - core, axis=1, keepdims=False)
    act_half = act_half.reshape(chips, local_experts, rows_here, quarter)
    act_other = act_other.reshape(chips, local_experts, rows_here, quarter)
    expert_out = jnp.einsum(
        "qerj,eqjd->erd", act_half, down_mine, preferred_element_type=jnp.float32
    ) + jnp.einsum("qerj,eqjd->erd", act_other, down_other, preferred_element_type=jnp.float32)
    expert_out = expert_out.astype(jnp.bfloat16).reshape(
        local_experts, owner_count, item_count, feat_width
    )
    returned = lax.all_to_all(expert_out, "expert", split_axis=1, concat_axis=1, tiled=True)
    flat_back = returned.reshape(slot_total, feat_width)
    combine = jnp.sum(
        jnp.where(
            slot_of[:, :, None] == slot_ids[None, None, :], gate_weights[:, :, None], 0.0
        ),
        axis=1,
    )
    mixture = jnp.dot(
        combine,
        flat_back.astype(jnp.float32),
        precision=lax.Precision.HIGHEST,
        preferred_element_type=jnp.float32,
    )
    updated = widened + mixture
    dest_hot = (next_device[:, None] == jnp.arange(owner_count, dtype=jnp.int32)[None, :]).astype(
        jnp.int32
    ) * survive[:, None]
    dest_before = jnp.cumsum(dest_hot, axis=0) - dest_hot
    handoff_pos = jnp.sum(dest_before * dest_hot, axis=1)
    hand_slot = jnp.where(survive > 0, next_device * hand_cap + handoff_pos, owner_count * hand_cap)
    row_plus = jnp.arange(row_count, dtype=jnp.int32) + 1
    target = (
        jnp.zeros((owner_count * hand_cap,), jnp.int32).at[hand_slot].set(row_plus, mode="drop")
    )
    stacked = jnp.concatenate([jnp.zeros((1, feat_width), jnp.float32), updated], axis=0)
    leaving = stacked[target].reshape(owner_count, hand_cap, feat_width)
    arrived = lax.all_to_all(leaving, "expert", split_axis=0, concat_axis=0, tiled=True)
    return arrived.reshape(owner_count * hand_cap, feat_width)


def solution(mesh):
    chips = mesh.shape["rep"] // 2
    split = Mesh(
        mesh.devices.reshape(chips, 2, mesh.shape["expert"]), ("ry", "rc", "expert")
    )
    rep = ("ry", "rc")
    in_specs = (
        P("expert", rep),
        P(rep),
        P("expert", None),
        P("expert"),
        P("expert", None),
        P("expert"),
        P("expert", rep, None),
        P("expert", None, rep),
    )
    out_specs = P("expert", rep)
    return jax.shard_map(
        per_device, mesh=split, in_specs=in_specs, out_specs=out_specs, check_vma=False
    )
```

```python
import jax
import jax.numpy as jnp
from jax import lax
from jax.sharding import Mesh, PartitionSpec as P


def per_device(
    tokens, norm_gain, gate_weights, exit_flags, routes, next_device, up_weight, down_weight
):
    row_count, feat_width = tokens.shape
    owner_count = lax.axis_size("expert")
    rep_count = lax.axis_size("ry") * lax.axis_size("rc")
    local_experts = up_weight.shape[0]
    hid = up_weight.shape[2]
    route_count = routes.shape[1]
    experts_all = local_experts * owner_count
    most_live = row_count // 2
    capacity = route_count * most_live // experts_all
    hand_cap = (most_live + owner_count - 1) // owner_count
    slot_total = local_experts * owner_count * capacity
    hid_part = hid // rep_count
    widened = tokens.astype(jnp.float32)
    survive = 1 - exit_flags
    hit = routes[:, :, None] == jnp.arange(experts_all, dtype=jnp.int32)[None, None, :]
    chosen = jnp.sum(hit.astype(jnp.float32), axis=1) * survive[:, None].astype(jnp.float32)
    gate_of = jnp.sum(jnp.where(hit, gate_weights[:, :, None], 0.0), axis=1)
    row_ids = jnp.arange(row_count, dtype=jnp.int32)
    before = (row_ids[:, None] > row_ids[None, :]).astype(jnp.bfloat16)
    count = jnp.dot(before, chosen.astype(jnp.bfloat16), preferred_element_type=jnp.float32)
    cap_ids = jnp.arange(capacity, dtype=jnp.float32)
    in_slot = chosen[:, :, None] * (count[:, :, None] == cap_ids[None, None, :]).astype(
        jnp.float32
    )
    in_slot = jnp.transpose(
        in_slot.reshape(row_count, owner_count, local_experts, capacity), (0, 2, 1, 3)
    ).reshape(row_count, slot_total)
    gate_slot = jnp.transpose(
        gate_of.reshape(row_count, owner_count, local_experts, 1), (0, 2, 1, 3)
    )
    gate_slot = jnp.broadcast_to(
        gate_slot, (row_count, local_experts, owner_count, capacity)
    ).reshape(row_count, slot_total)
    squares = jnp.sum(widened * widened, axis=1)
    spread = jnp.broadcast_to(squares[None], (rep_count,) + squares.shape)
    squares = jnp.sum(lax.all_to_all(spread, ("ry", "rc"), 0, 0, tiled=True), axis=0)
    rinv_rows = lax.rsqrt(squares / (feat_width * rep_count) + 1e-06)
    normed = (widened * rinv_rows[:, None] * norm_gain[None, :]).astype(jnp.bfloat16)
    pick = jnp.transpose(in_slot).astype(jnp.bfloat16)
    outbound = jnp.dot(pick, normed, preferred_element_type=jnp.float32).astype(jnp.bfloat16)
    outbound = outbound.reshape(local_experts, owner_count, capacity, feat_width)
    received = lax.all_to_all(outbound, "expert", split_axis=1, concat_axis=1, tiled=True)
    item_count = received.shape[2]
    rows_here = owner_count * item_count
    flattened = received.reshape(local_experts, rows_here, feat_width)
    partial_value = jnp.einsum(
        "erd,edh->erh", flattened, up_weight, preferred_element_type=jnp.float32
    )
    core = lax.axis_index("rc")
    sibling = [(i, 1 - i) for i in range(2)]
    chips = lax.axis_size("ry")
    quarter = hid // (2 * chips)
    pieces = partial_value.reshape(local_experts * rows_here, 2 * chips, quarter)
    pieces = jnp.transpose(pieces, (1, 0, 2)).reshape(2, chips, local_experts * rows_here, quarter)
    mine = lax.dynamic_index_in_dim(pieces, core, axis=0, keepdims=False)
    theirs = lax.dynamic_index_in_dim(pieces, 1 - core, axis=0, keepdims=False)
    half_sum = mine + lax.ppermute(theirs, "rc", sibling)
    got = lax.all_to_all(half_sum, "ry", split_axis=0, concat_axis=0, tiled=True)
    hidden_part = jnp.sum(got, axis=0)
    act_part = jax.nn.silu(hidden_part).astype(jnp.bfloat16)
    act_tile = jnp.broadcast_to(act_part[None], (chips,) + act_part.shape)
    act_half = lax.all_to_all(act_tile, "ry", split_axis=0, concat_axis=0, tiled=True)
    act_other = lax.ppermute(act_half, "rc", sibling)
    down_q = down_weight.reshape(local_experts, 2, chips, quarter, feat_width)
    down_mine = lax.dynamic_index_in_dim(down_q, core, axis=1, keepdims=False)
    down_other = lax.dynamic_index_in_dim(down_q, 1 - core, axis=1, keepdims=False)
    act_half = act_half.reshape(chips, local_experts, rows_here, quarter)
    act_other = act_other.reshape(chips, local_experts, rows_here, quarter)
    expert_out = jnp.einsum(
        "qerj,eqjd->erd", act_half, down_mine, preferred_element_type=jnp.float32
    ) + jnp.einsum("qerj,eqjd->erd", act_other, down_other, preferred_element_type=jnp.float32)
    expert_out = expert_out.astype(jnp.bfloat16).reshape(
        local_experts, owner_count, item_count, feat_width
    )
    returned = lax.all_to_all(expert_out, "expert", split_axis=1, concat_axis=1, tiled=True)
    flat_back = returned.reshape(slot_total, feat_width)
    combine = in_slot * gate_slot
    mixture = jnp.dot(
        combine,
        flat_back.astype(jnp.float32),
        precision=lax.Precision.HIGHEST,
        preferred_element_type=jnp.float32,
    )
    updated = widened + mixture
    dest_hot = (next_device[:, None] == jnp.arange(owner_count, dtype=jnp.int32)[None, :]).astype(
        jnp.int32
    ) * survive[:, None]
    dest_before = jnp.cumsum(dest_hot, axis=0) - dest_hot
    handoff_pos = jnp.sum(dest_before * dest_hot, axis=1)
    hand_slot = jnp.where(survive > 0, next_device * hand_cap + handoff_pos, owner_count * hand_cap)
    row_plus = jnp.arange(row_count, dtype=jnp.int32) + 1
    target = (
        jnp.zeros((owner_count * hand_cap,), jnp.int32).at[hand_slot].set(row_plus, mode="drop")
    )
    stacked = jnp.concatenate([jnp.zeros((1, feat_width), jnp.float32), updated], axis=0)
    leaving = stacked[target].reshape(owner_count, hand_cap, feat_width)
    arrived = lax.all_to_all(leaving, "expert", split_axis=0, concat_axis=0, tiled=True)
    return arrived.reshape(owner_count * hand_cap, feat_width)


def solution(mesh):
    chips = mesh.shape["rep"] // 2
    split = Mesh(
        mesh.devices.reshape(chips, 2, mesh.shape["expert"]), ("ry", "rc", "expert")
    )
    rep = ("ry", "rc")
    in_specs = (
        P("expert", rep),
        P(rep),
        P("expert", None),
        P("expert"),
        P("expert", None),
        P("expert"),
        P("expert", rep, None),
        P("expert", None, rep),
    )
    out_specs = P("expert", rep)
    return jax.shard_map(
        per_device, mesh=split, in_specs=in_specs, out_specs=out_specs, check_vma=False
    )
```

```python
import jax
import jax.numpy as jnp
from jax import lax
from jax.sharding import Mesh, PartitionSpec as P


def per_device(
    tokens, norm_gain, gate_weights, exit_flags, routes, next_device, up_weight, down_weight
):
    row_count, feat_width = tokens.shape
    owner_count = lax.axis_size("expert")
    rep_count = lax.axis_size("ry") * lax.axis_size("rc")
    local_experts = up_weight.shape[0]
    hid = up_weight.shape[2]
    route_count = routes.shape[1]
    experts_all = local_experts * owner_count
    most_live = row_count // 2
    capacity = route_count * most_live // experts_all
    hand_cap = (most_live + owner_count - 1) // owner_count
    slot_total = local_experts * owner_count * capacity
    hid_part = hid // rep_count
    widened = tokens.astype(jnp.float32)
    survive = 1 - exit_flags
    pair_live = jnp.repeat(survive, route_count)
    route_flat = routes.reshape(-1)
    one_hot = (route_flat[:, None] == jnp.arange(experts_all, dtype=jnp.int32)[None, :]).astype(
        jnp.int32
    ) * pair_live[:, None]
    earlier = jnp.cumsum(one_hot, axis=0) - one_hot
    position = jnp.sum(earlier * one_hot, axis=1)
    owner_id = route_flat // local_experts
    local_id = route_flat % local_experts
    slot_index = (local_id * owner_count + owner_id) * capacity + position
    slot_index = jnp.where(pair_live > 0, slot_index, slot_total)
    squares = jnp.sum(widened * widened, axis=1)
    spread = jnp.broadcast_to(squares[None], (rep_count,) + squares.shape)
    squares = jnp.sum(lax.all_to_all(spread, ("ry", "rc"), 0, 0, tiled=True), axis=0)
    rinv_rows = lax.rsqrt(squares / (feat_width * rep_count) + 1e-06)
    normed = (widened * rinv_rows[:, None] * norm_gain[None, :]).astype(jnp.bfloat16)
    slot_ids = jnp.arange(slot_total, dtype=jnp.int32)
    slot_of = slot_index.reshape(row_count, route_count)
    pick = jnp.sum(
        (slot_of[None, :, :] == slot_ids[:, None, None]).astype(jnp.float32), axis=2
    ).astype(jnp.bfloat16)
    outbound = jnp.dot(pick, normed, preferred_element_type=jnp.float32).astype(jnp.bfloat16)
    outbound = outbound.reshape(local_experts, owner_count, capacity, feat_width)
    received = lax.all_to_all(outbound, "expert", split_axis=1, concat_axis=1, tiled=True)
    item_count = received.shape[2]
    rows_here = owner_count * item_count
    flattened = received.reshape(local_experts, rows_here, feat_width)
    core = lax.axis_index("rc")
    sibling = [(i, 1 - i) for i in range(2)]
    chips = lax.axis_size("ry")
    quarter = hid // (2 * chips)
    up_q = up_weight.reshape(local_experts, feat_width, 2, chips, quarter)
    up_theirs = lax.dynamic_index_in_dim(up_q, 1 - core, axis=2, keepdims=False)
    up_mine = lax.dynamic_index_in_dim(up_q, core, axis=2, keepdims=False)
    theirs = jnp.einsum(
        "erd,edqj->qerj", flattened, up_theirs, preferred_element_type=jnp.float32
    ).reshape(chips, local_experts * rows_here, quarter)
    mine = jnp.einsum(
        "erd,edqj->qerj", flattened, up_mine, preferred_element_type=jnp.float32
    ).reshape(chips, local_experts * rows_here, quarter)
    half_sum = mine + lax.ppermute(theirs, "rc", sibling)
    got = lax.all_to_all(half_sum, "ry", split_axis=0, concat_axis=0, tiled=True)
    hidden_part = jnp.sum(got, axis=0)
    act_part = jax.nn.silu(hidden_part).astype(jnp.bfloat16)
    act_tile = jnp.broadcast_to(act_part[None], (chips,) + act_part.shape)
    act_half = lax.all_to_all(act_tile, "ry", split_axis=0, concat_axis=0, tiled=True)
    act_other = lax.ppermute(act_half, "rc", sibling)
    down_q = down_weight.reshape(local_experts, 2, chips, quarter, feat_width)
    down_mine = lax.dynamic_index_in_dim(down_q, core, axis=1, keepdims=False)
    down_other = lax.dynamic_index_in_dim(down_q, 1 - core, axis=1, keepdims=False)
    act_half = act_half.reshape(chips, local_experts, rows_here, quarter)
    act_other = act_other.reshape(chips, local_experts, rows_here, quarter)
    expert_out = jnp.einsum(
        "qerj,eqjd->erd", act_half, down_mine, preferred_element_type=jnp.float32
    ) + jnp.einsum("qerj,eqjd->erd", act_other, down_other, preferred_element_type=jnp.float32)
    expert_out = expert_out.astype(jnp.bfloat16).reshape(
        local_experts, owner_count, item_count, feat_width
    )
    returned = lax.all_to_all(expert_out, "expert", split_axis=1, concat_axis=1, tiled=True)
    flat_back = returned.reshape(slot_total, feat_width)
    combine = jnp.sum(
        jnp.where(
            slot_of[:, :, None] == slot_ids[None, None, :], gate_weights[:, :, None], 0.0
        ),
        axis=1,
    )
    mixture = jnp.dot(
        combine,
        flat_back.astype(jnp.float32),
        precision=lax.Precision.HIGHEST,
        preferred_element_type=jnp.float32,
    )
    updated = widened + mixture
    dest_hot = (next_device[:, None] == jnp.arange(owner_count, dtype=jnp.int32)[None, :]).astype(
        jnp.int32
    ) * survive[:, None]
    dest_before = jnp.cumsum(dest_hot, axis=0) - dest_hot
    handoff_pos = jnp.sum(dest_before * dest_hot, axis=1)
    hand_slot = jnp.where(survive > 0, next_device * hand_cap + handoff_pos, owner_count * hand_cap)
    row_plus = jnp.arange(row_count, dtype=jnp.int32) + 1
    target = (
        jnp.zeros((owner_count * hand_cap,), jnp.int32).at[hand_slot].set(row_plus, mode="drop")
    )
    stacked = jnp.concatenate([jnp.zeros((1, feat_width), jnp.float32), updated], axis=0)
    leaving = stacked[target].reshape(owner_count, hand_cap, feat_width)
    arrived = lax.all_to_all(leaving, "expert", split_axis=0, concat_axis=0, tiled=True)
    return arrived.reshape(owner_count * hand_cap, feat_width)


def solution(mesh):
    chips = mesh.shape["rep"] // 2
    split = Mesh(
        mesh.devices.reshape(chips, 2, mesh.shape["expert"]), ("ry", "rc", "expert")
    )
    rep = ("ry", "rc")
    in_specs = (
        P("expert", rep),
        P(rep),
        P("expert", None),
        P("expert"),
        P("expert", None),
        P("expert"),
        P("expert", rep, None),
        P("expert", None, rep),
    )
    out_specs = P("expert", rep)
    return jax.shard_map(
        per_device, mesh=split, in_specs=in_specs, out_specs=out_specs, check_vma=False
    )
```

```python
import jax
import jax.numpy as jnp
from jax import lax
from jax.sharding import Mesh, PartitionSpec as P


def per_device(
    tokens, norm_gain, gate_weights, exit_flags, routes, next_device, up_weight, down_weight
):
    row_count, feat_width = tokens.shape
    owner_count = lax.axis_size("expert")
    rep_count = lax.axis_size("ry") * lax.axis_size("rc")
    local_experts = up_weight.shape[0]
    hid = up_weight.shape[2]
    route_count = routes.shape[1]
    experts_all = local_experts * owner_count
    most_live = row_count // 2
    capacity = route_count * most_live // experts_all
    hand_cap = (most_live + owner_count - 1) // owner_count
    slot_total = local_experts * owner_count * capacity
    hid_part = hid // rep_count
    widened = tokens.astype(jnp.float32)
    survive = 1 - exit_flags
    pair_live = jnp.repeat(survive, route_count)
    route_flat = routes.reshape(-1)
    one_hot = (route_flat[:, None] == jnp.arange(experts_all, dtype=jnp.int32)[None, :]).astype(
        jnp.int32
    ) * pair_live[:, None]
    earlier = jnp.cumsum(one_hot, axis=0) - one_hot
    position = jnp.sum(earlier * one_hot, axis=1)
    owner_id = route_flat // local_experts
    local_id = route_flat % local_experts
    slot_index = (local_id * owner_count + owner_id) * capacity + position
    slot_index = jnp.where(pair_live > 0, slot_index, slot_total)
    squares = jnp.sum(widened * widened, axis=1)
    spread = jnp.broadcast_to(squares[None], (rep_count,) + squares.shape)
    squares = jnp.sum(lax.all_to_all(spread, ("ry", "rc"), 0, 0, tiled=True), axis=0)
    rinv_rows = lax.rsqrt(squares / (feat_width * rep_count) + 1e-06)
    normed = (widened * rinv_rows[:, None] * norm_gain[None, :]).astype(jnp.bfloat16)
    slot_ids = jnp.arange(slot_total, dtype=jnp.int32)
    slot_of = slot_index.reshape(row_count, route_count)
    pick = jnp.sum(
        (slot_of[None, :, :] == slot_ids[:, None, None]).astype(jnp.float32), axis=2
    ).astype(jnp.bfloat16)
    pick = jnp.transpose(
        pick.reshape(local_experts, owner_count, capacity, row_count), (1, 0, 2, 3)
    ).reshape(slot_total, row_count)
    outbound = jnp.dot(pick, normed, preferred_element_type=jnp.float32).astype(jnp.bfloat16)
    outbound = jnp.transpose(
        outbound.reshape(owner_count, local_experts, capacity, feat_width), (1, 0, 2, 3)
    )
    received = lax.all_to_all(outbound, "expert", split_axis=1, concat_axis=1, tiled=True)
    item_count = received.shape[2]
    rows_here = owner_count * item_count
    flattened = received.reshape(local_experts, rows_here, feat_width)
    partial_value = jnp.einsum(
        "erd,edh->erh", flattened, up_weight, preferred_element_type=jnp.float32
    )
    core = lax.axis_index("rc")
    sibling = [(i, 1 - i) for i in range(2)]
    chips = lax.axis_size("ry")
    quarter = hid // (2 * chips)
    pieces = partial_value.reshape(local_experts * rows_here, 2 * chips, quarter)
    pieces = jnp.transpose(pieces, (1, 0, 2)).reshape(2, chips, local_experts * rows_here, quarter)
    mine = lax.dynamic_index_in_dim(pieces, core, axis=0, keepdims=False)
    theirs = lax.dynamic_index_in_dim(pieces, 1 - core, axis=0, keepdims=False)
    half_sum = mine + lax.ppermute(theirs, "rc", sibling)
    got = lax.all_to_all(half_sum, "ry", split_axis=0, concat_axis=0, tiled=True)
    hidden_part = jnp.sum(got, axis=0)
    act_part = jax.nn.silu(hidden_part).astype(jnp.bfloat16)
    act_tile = jnp.broadcast_to(act_part[None], (chips,) + act_part.shape)
    act_half = lax.all_to_all(act_tile, "ry", split_axis=0, concat_axis=0, tiled=True)
    act_other = lax.ppermute(act_half, "rc", sibling)
    down_q = down_weight.reshape(local_experts, 2, chips, quarter, feat_width)
    down_mine = lax.dynamic_index_in_dim(down_q, core, axis=1, keepdims=False)
    down_other = lax.dynamic_index_in_dim(down_q, 1 - core, axis=1, keepdims=False)
    act_half = act_half.reshape(chips, local_experts, rows_here, quarter)
    act_other = act_other.reshape(chips, local_experts, rows_here, quarter)
    act_half = act_half.reshape(chips, local_experts, owner_count, item_count, quarter)
    act_other = act_other.reshape(chips, local_experts, owner_count, item_count, quarter)
    expert_out = jnp.einsum(
        "qeocj,eqjd->oecd", act_half, down_mine, preferred_element_type=jnp.float32
    ) + jnp.einsum("qeocj,eqjd->oecd", act_other, down_other, preferred_element_type=jnp.float32)
    expert_out = jnp.transpose(expert_out.astype(jnp.bfloat16), (1, 0, 2, 3))
    returned = lax.all_to_all(expert_out, "expert", split_axis=1, concat_axis=1, tiled=True)
    flat_back = returned.reshape(slot_total, feat_width)
    combine = jnp.sum(
        jnp.where(
            slot_of[:, :, None] == slot_ids[None, None, :], gate_weights[:, :, None], 0.0
        ),
        axis=1,
    )
    mixture = jnp.dot(
        combine,
        flat_back.astype(jnp.float32),
        precision=lax.Precision.HIGHEST,
        preferred_element_type=jnp.float32,
    )
    updated = widened + mixture
    dest_hot = (next_device[:, None] == jnp.arange(owner_count, dtype=jnp.int32)[None, :]).astype(
        jnp.int32
    ) * survive[:, None]
    dest_before = jnp.cumsum(dest_hot, axis=0) - dest_hot
    handoff_pos = jnp.sum(dest_before * dest_hot, axis=1)
    hand_slot = jnp.where(survive > 0, next_device * hand_cap + handoff_pos, owner_count * hand_cap)
    row_plus = jnp.arange(row_count, dtype=jnp.int32) + 1
    target = (
        jnp.zeros((owner_count * hand_cap,), jnp.int32).at[hand_slot].set(row_plus, mode="drop")
    )
    stacked = jnp.concatenate([jnp.zeros((1, feat_width), jnp.float32), updated], axis=0)
    leaving = stacked[target].reshape(owner_count, hand_cap, feat_width)
    arrived = lax.all_to_all(leaving, "expert", split_axis=0, concat_axis=0, tiled=True)
    return arrived.reshape(owner_count * hand_cap, feat_width)


def solution(mesh):
    chips = mesh.shape["rep"] // 2
    split = Mesh(
        mesh.devices.reshape(chips, 2, mesh.shape["expert"]), ("ry", "rc", "expert")
    )
    rep = ("ry", "rc")
    in_specs = (
        P("expert", rep),
        P(rep),
        P("expert", None),
        P("expert"),
        P("expert", None),
        P("expert"),
        P("expert", rep, None),
        P("expert", None, rep),
    )
    out_specs = P("expert", rep)
    return jax.shard_map(
        per_device, mesh=split, in_specs=in_specs, out_specs=out_specs, check_vma=False
    )
```
